32 devices in a mesh: ctx: 8 (over y, x, core), tp: 4 (over z).
Axes of the slice: x: 2, y: 2, z: 4, core: 2. Of those that a mesh axis runs over, the one named last changes fastest.
Arguments:
- queries: bfloat16 [1024, 4096], P('ctx', 'tp'), may hold values from -128 to 128
- key_rows: bfloat16 [1024, 4096], P('ctx', 'tp'), may hold values from -6 to 6
- value_rows: bfloat16 [1024, 4096], P('ctx', 'tp'), may hold values from -6 to 6
- view_mask: int32 [8, 3], replicated, may hold values from 0 to 1, as said below
- norm_gain: float32 [4096], replicated, may hold values from 0.5 to 1.5
- normed_grad: bfloat16 [1024, 4096], P(('ctx', 'tp')), may hold values from -6 to 6
Outputs:
- normed: bfloat16 [1024, 4096], P(('ctx', 'tp'))
- query_grad: bfloat16 [1024, 4096], P('ctx', 'tp')
- key_grad: bfloat16 [1024, 4096], P('ctx', 'tp')
- value_grad: bfloat16 [1024, 4096], P('ctx', 'tp')
The draws below stay inside these ranges and needn't reach their ends.
Inputs may be any that keep to these rules, and one draw needn't show every extreme that they name: `view_mask`: the blocks form views of consecutive blocks. Block 0 begins a view; otherwise a view begins only at blocks b with b % 4 equal to 2 or 3, and in every group of 4 blocks at least one of these two begins a view. A column is 1 exactly where its key block lies inside the grid of blocks and either is not later than the query block or lies in the query block's view.
All inputs are finite; a program needn't handle non-finite values.
Results may differ from the reference program's by a relative error of at most 0.012.
Values may be sent and summed in bfloat16 or wider, within the bound.
No kernel may reach another device: no remote copies, remote signals or barrier semaphores. Data moves between devices by JAX's collectives and lax.ppermute only.
A program may use at most 64 MiB of HBM per device.

```python
import jax
import jax.numpy as jnp
from jax import lax

HEADS = 32
HSZ = 128
D = 4096
TOK_DEV = 128
REACH = 2
VIEW_BLOCKS = 4
BLOCKS = 8
TOKENS = 1024


def paired_rows(key):
    base_keys = jnp.clip(jax.random.normal(jax.random.fold_in(key, 11), (TOKENS, D), jnp.float32), -5.0, 5.0)
    base_queries = jnp.clip(jax.random.normal(jax.random.fold_in(key, 12), (TOKENS, D), jnp.float32), -5.0, 5.0)
    return (base_queries, base_keys)


def draw_queries(key, part):
    return paired_rows(key)[0].astype(jnp.bfloat16)


def draw_key_rows(key, part):
    return paired_rows(key)[1].astype(jnp.bfloat16)


def draw_view_mask(key, part):
    span_blocks = 2 * REACH - 1
    block_ids = jnp.arange(BLOCKS, dtype=jnp.int32)
    groups = BLOCKS // VIEW_BLOCKS
    kinds = jax.random.randint(jax.random.fold_in(key, 21), (groups,), 0, 3)
    block_kind = jnp.repeat(kinds, VIEW_BLOCKS)
    offset = block_ids % VIEW_BLOCKS
    begins = (block_ids == 0) | (offset == 2) & (block_kind != 1) | (offset == 3) & (block_kind != 0)
    starts = jnp.where(begins, 1, 0).astype(jnp.int32)
    view_ids = jnp.cumsum(starts) - 1
    row_ids = block_ids[:, None]
    column_ids = jnp.arange(span_blocks, dtype=jnp.int32)[None, :]
    target = row_ids + column_ids - (REACH - 1)
    inside = (target >= 0) & (target < BLOCKS)
    clipped = jnp.clip(target, 0, BLOCKS - 1)
    same_view = view_ids[clipped] == view_ids[row_ids]
    later = column_ids > REACH - 1
    live = inside & (jnp.logical_not(later) | same_view)
    return jnp.where(live, 1, 0).astype(jnp.int32)


def steps_of(stream_key, dims, shards, smallest, top_value):
    level, own = 1.0, jax.random.fold_in(stream_key, 6)
    for dim, blocks in shards:
        draws = jnp.exp(jax.random.uniform(jax.random.fold_in(own, dim), (blocks,), jnp.float32, smallest / len(shards), top_value / len(shards)))
        level = level * jnp.repeat(draws, dims[dim] // blocks).reshape([-1 if axis == dim else 1 for axis in range(len(dims))])
    return level


def centred(stream_key, extent, spread, most, pieces=(), kind=jnp.bfloat16):
    drawn = jax.random.normal(stream_key, extent, jnp.float32) * spread
    if len(pieces) > 0:
        drawn = steps_of(stream_key, extent, pieces, -0.22, 0.18) * drawn
    return jnp.clip(drawn, min=-most, max=most).astype(kind)


def setup_inputs(seed: int = 0) -> dict:
    arg_keys = jax.random.split(jax.random.key(seed), 7)
    queries = draw_queries(jax.random.fold_in(arg_keys[6], 71), 0)
    key_rows = draw_key_rows(jax.random.fold_in(arg_keys[6], 71), 0)
    value_rows = centred(arg_keys[2], (TOKENS, D), 1.0, 6.0, ((0, 8), (1, 4)))
    view_mask = draw_view_mask(jax.random.fold_in(arg_keys[6], 71), 0)
    norm_gain = jnp.clip(1.0 + 0.1 * jax.random.normal(arg_keys[4], (D,), jnp.float32), 0.5, 1.5)
    normed_grad = centred(arg_keys[5], (TOKENS, D), 1.0, 6.0, ((0, 32),))
    return dict(queries=queries, key_rows=key_rows, value_rows=value_rows, view_mask=view_mask, norm_gain=norm_gain, normed_grad=normed_grad)


NEGATIVE = -1e+30
EPSILON = 1e-06

def low_round(values):
    return lax.optimization_barrier(values.astype(jnp.bfloat16)).astype(jnp.float32)

def reference(queries, key_rows, value_rows, view_mask, norm_gain, normed_grad):
    span_blocks = 2 * REACH - 1
    rim_rows = (REACH - 1) * TOK_DEV
    score_scale = HSZ ** (-0.5)
    q_heads = queries.reshape(TOKENS, HEADS, HSZ)
    k_heads = key_rows.reshape(TOKENS, HEADS, HSZ)
    v_heads = value_rows.reshape(TOKENS, HEADS, HSZ)
    pad_width = ((rim_rows, rim_rows), (0, 0), (0, 0))
    k_padded = jnp.pad(k_heads, pad_width)
    v_padded = jnp.pad(v_heads, pad_width)
    block_list = jnp.arange(BLOCKS, dtype=jnp.int32)

    def window_probs(which):
        start = (which * TOK_DEV).astype(jnp.int32)
        q_block = lax.dynamic_slice_in_dim(q_heads, start, TOK_DEV, 0)
        k_window = lax.dynamic_slice_in_dim(k_padded, start, span_blocks * TOK_DEV, 0)
        v_window = lax.dynamic_slice_in_dim(v_padded, start, span_blocks * TOK_DEV, 0)
        live = jnp.repeat(view_mask[which], TOK_DEV) > 0
        scores = jnp.einsum('thd,shd->hts', q_block.astype(jnp.float32), k_window.astype(jnp.float32)) * score_scale
        scores = jnp.where(live[None, None, :], scores, NEGATIVE)
        peak = lax.optimization_barrier(jnp.max(scores, -1, keepdims=True))
        log_total = peak + jnp.log(lax.optimization_barrier(jnp.sum(jnp.exp(scores - peak), -1, keepdims=True)))
        return (k_window, v_window, jnp.exp(scores - log_total), log_total[:, :, 0])

    def forward(which):
        k_window, v_window, probs, log_total = window_probs(which)
        out_block = jnp.einsum('hts,shd->thd', low_round(probs), v_window.astype(jnp.float32)).astype(jnp.bfloat16)
        return (out_block, log_total)
    out_blocks, totals = lax.map(forward, block_list)
    attended = out_blocks.reshape(TOKENS, D)
    values_f = attended.astype(jnp.float32)
    inverse = lax.rsqrt(lax.optimization_barrier(jnp.mean(values_f * values_f, -1, keepdims=True)) + EPSILON)
    gain_row = norm_gain.astype(jnp.float32)
    normed = (values_f * inverse * gain_row).astype(jnp.bfloat16)
    upstream = normed_grad.astype(jnp.float32) * gain_row
    inner_mean = lax.optimization_barrier(jnp.mean(upstream * values_f, -1, keepdims=True))
    attended_grad = (inverse * upstream - values_f * inverse * inverse * inverse * inner_mean).astype(jnp.bfloat16)
    grad_heads = attended_grad.reshape(TOKENS, HEADS, HSZ)
    out_heads = attended.reshape(TOKENS, HEADS, HSZ)
    delta = lax.optimization_barrier(jnp.sum(grad_heads.astype(jnp.float32) * out_heads.astype(jnp.float32), -1))

    def query_side(which):
        start = (which * TOK_DEV).astype(jnp.int32)
        k_window, v_window, probs, log_total = window_probs(which)
        grad_block = lax.dynamic_slice_in_dim(grad_heads, start, TOK_DEV, 0)
        delta_block = lax.dynamic_slice_in_dim(delta, start, TOK_DEV, 0).T
        prob_grad = jnp.einsum('thd,shd->hts', grad_block.astype(jnp.float32), v_window.astype(jnp.float32))
        score_grad = low_round(probs * (prob_grad - delta_block[:, :, None]))
        result = jnp.einsum('hts,shd->thd', score_grad, k_window.astype(jnp.float32)) * score_scale
        return result.astype(jnp.bfloat16)
    query_grad = lax.map(query_side, block_list).reshape(TOKENS, D)
    q_padded = jnp.pad(q_heads, pad_width)
    grad_padded = jnp.pad(grad_heads, pad_width)
    total_rows = jnp.transpose(totals, (0, 2, 1)).reshape(TOKENS, HEADS)
    total_padded = jnp.pad(total_rows, ((rim_rows, rim_rows), (0, 0)))
    delta_padded = jnp.pad(delta, ((rim_rows, rim_rows), (0, 0)))
    mask_padded = jnp.pad(view_mask, ((REACH - 1, REACH - 1), (0, 0)))

    def key_side(which):
        start = (which * TOK_DEV).astype(jnp.int32)
        k_block = lax.dynamic_slice_in_dim(k_heads, start, TOK_DEV, 0).astype(jnp.float32)
        v_block = lax.dynamic_slice_in_dim(v_heads, start, TOK_DEV, 0).astype(jnp.float32)
        q_window = lax.dynamic_slice_in_dim(q_padded, start, span_blocks * TOK_DEV, 0).astype(jnp.float32)
        grad_window = lax.dynamic_slice_in_dim(grad_padded, start, span_blocks * TOK_DEV, 0).astype(jnp.float32)
        total_window = lax.dynamic_slice_in_dim(total_padded, start, span_blocks * TOK_DEV, 0).T
        delta_window = lax.dynamic_slice_in_dim(delta_padded, start, span_blocks * TOK_DEV, 0).T
        mask_rows = lax.dynamic_slice_in_dim(mask_padded, which, span_blocks, 0)
        query_live = jnp.repeat(jnp.diagonal(jnp.flip(mask_rows, 1)), TOK_DEV) > 0
        scores = jnp.einsum('qhd,khd->hqk', q_window, k_block) * score_scale
        scores = jnp.where(query_live[None, :, None], scores, NEGATIVE)
        probs = jnp.exp(scores - total_window[:, :, None])
        prob_grad = jnp.einsum('qhd,khd->hqk', grad_window, v_block)
        score_grad = low_round(probs * (prob_grad - delta_window[:, :, None]))
        key_part = (jnp.einsum('hqk,qhd->khd', score_grad, q_window) * score_scale).astype(jnp.bfloat16)
        value_part = jnp.einsum('hqk,qhd->khd', low_round(probs), grad_window).astype(jnp.bfloat16)
        return (key_part, value_part)
    key_parts, value_parts = lax.map(key_side, block_list)
    return (normed, query_grad, key_parts.reshape(TOKENS, D), value_parts.reshape(TOKENS, D))
```

```python
import jax
import jax.numpy as jnp
from jax import lax
from jax.sharding import PartitionSpec as P

HSZ = 128
REACH = 2


NEGATIVE = -1e30
EPSILON = 1e-06
STATS_SUM = "a2a"


def passed_along(x, axis, by):
    peers = lax.axis_size(axis)
    pairs = [(i, i + by) for i in range(peers) if 0 <= i + by < peers]
    return lax.ppermute(x, axis, pairs)


def split_heads(values):
    return values.reshape(values.shape[0], -1, HSZ)


def tp_sum(stats):
    if STATS_SUM == "psum":
        return lax.psum(stats, "tp")
    peers = lax.axis_size("tp")
    if STATS_SUM == "a2a":
        spread = jnp.broadcast_to(stats[None], (peers,) + stats.shape)
        gathered = lax.all_to_all(spread, "tp", split_axis=0, concat_axis=0, tiled=True)
        return jnp.sum(gathered, 0)
    total = stats
    for shift in range(1, peers):
        total = total + lax.ppermute(stats, "tp", [(i, (i + shift) % peers) for i in range(peers)])
    return total


def per_device(queries, key_rows, value_rows, view_mask, norm_gain, normed_grad):
    length = queries.shape[0]
    width = queries.shape[1]
    features = norm_gain.shape[0]
    span_blocks = 2 * REACH - 1
    score_scale = HSZ ** (-0.5)
    position = lax.axis_index("ctx")
    part = lax.axis_index("tp")

    grad_tiles = lax.all_to_all(normed_grad, "tp", split_axis=1, concat_axis=0, tiled=True)
    gain_local = lax.dynamic_slice_in_dim(norm_gain, part * width, width, 0)

    both = jnp.concatenate([key_rows, value_rows], axis=1)
    from_prev = passed_along(both, "ctx", 1)
    from_next = passed_along(both, "ctx", -1)
    key_ext = jnp.concatenate([from_prev[:, :width], key_rows, from_next[:, :width]], axis=0)
    value_ext = jnp.concatenate([from_prev[:, width:], value_rows, from_next[:, width:]], axis=0)

    mask_row = lax.dynamic_slice_in_dim(view_mask, position, 1, 0)[0]
    key_live = jnp.repeat(mask_row, length) > 0
    q_heads = split_heads(queries)
    k_heads = split_heads(key_ext)
    v_heads = split_heads(value_ext)
    scores = (
        jnp.einsum("thd,shd->hts", q_heads, k_heads, preferred_element_type=jnp.float32)
        * score_scale
    )
    scores = jnp.where(key_live[None, None, :], scores, NEGATIVE)
    peak = jnp.max(scores, -1, keepdims=True)
    log_total = peak + jnp.log(jnp.sum(jnp.exp(scores - peak), -1, keepdims=True))
    probs = jnp.exp(scores - log_total)
    probs_low = probs.astype(jnp.bfloat16)
    out_heads = jnp.einsum(
        "hts,shd->thd", probs_low, v_heads, preferred_element_type=jnp.float32
    ).astype(jnp.bfloat16)
    attended = out_heads.reshape(length, -1)

    values_f = attended.astype(jnp.float32)
    upstream = grad_tiles.astype(jnp.float32) * gain_local
    partial = jnp.stack(
        [jnp.sum(values_f * values_f, -1), jnp.sum(upstream * values_f, -1)], axis=-1
    )
    totals = tp_sum(partial)
    inverse = lax.rsqrt(totals[:, 0:1] / features + EPSILON)
    inner_mean = totals[:, 1:2] / features
    normed_heads = (values_f * inverse * gain_local).astype(jnp.bfloat16)
    normed = lax.all_to_all(normed_heads, "tp", split_axis=0, concat_axis=1, tiled=True)
    attended_grad = (
        inverse * upstream - values_f * inverse * inverse * inverse * inner_mean
    ).astype(jnp.bfloat16)

    grad_heads = split_heads(attended_grad)
    delta = jnp.sum(grad_heads.astype(jnp.float32) * out_heads.astype(jnp.float32), -1)
    prob_grad = jnp.einsum("thd,shd->hts", grad_heads, v_heads, preferred_element_type=jnp.float32)
    score_grad = (probs * (prob_grad - delta.T[:, :, None])).astype(jnp.bfloat16)
    query_grad = (
        (
            jnp.einsum("hts,shd->thd", score_grad, k_heads, preferred_element_type=jnp.float32)
            * score_scale
        )
        .astype(jnp.bfloat16)
        .reshape(length, -1)
    )
    key_terms = (
        jnp.einsum("hts,thd->shd", score_grad, q_heads, preferred_element_type=jnp.float32)
        * score_scale
    ).reshape(span_blocks * length, -1)
    value_terms = jnp.einsum(
        "hts,thd->shd", probs_low, grad_heads, preferred_element_type=jnp.float32
    ).reshape(span_blocks * length, -1)
    terms = jnp.concatenate([key_terms, value_terms], axis=1)
    total = terms[length : 2 * length]
    to_prev = terms[:length].astype(jnp.bfloat16)
    to_next = terms[2 * length :].astype(jnp.bfloat16)
    total = total + passed_along(to_prev, "ctx", -1).astype(jnp.float32)
    total = total + passed_along(to_next, "ctx", 1).astype(jnp.float32)
    total = total.astype(jnp.bfloat16)
    return (normed, query_grad, total[:, :width], total[:, width:])


def solution(mesh):
    placed = (P("ctx", "tp"), P("ctx", "tp"), P("ctx", "tp"), P(), P(), P(("ctx", "tp"), None))
    return jax.shard_map(
        per_device,
        mesh=mesh,
        in_specs=placed,
        out_specs=(P(("ctx", "tp"), None), P("ctx", "tp"), P("ctx", "tp"), P("ctx", "tp")),
        check_vma=False,
    )
```

```python
import jax
import jax.numpy as jnp
from jax import lax
from jax.sharding import PartitionSpec as P

HSZ = 128
REACH = 2


NEGATIVE = -1e30
EPSILON = 1e-06
STATS_SUM = "perm"
NG_MODE = "perm"
OUT_MODE = "perm"


def passed_along(x, axis, by):
    peers = lax.axis_size(axis)
    pairs = [(i, i + by) for i in range(peers) if 0 <= i + by < peers]
    return lax.ppermute(x, axis, pairs)


def split_heads(values):
    return values.reshape(values.shape[0], -1, HSZ)


def tp_sum(stats):
    if STATS_SUM == "psum":
        return lax.psum(stats, "tp")
    peers = lax.axis_size("tp")
    if STATS_SUM == "a2a":
        spread = jnp.broadcast_to(stats[None], (peers,) + stats.shape)
        gathered = lax.all_to_all(spread, "tp", split_axis=0, concat_axis=0, tiled=True)
        return jnp.sum(gathered, 0)
    total = stats
    for shift in range(1, peers):
        total = total + lax.ppermute(stats, "tp", [(i, (i + shift) % peers) for i in range(peers)])
    return total


def rolled(pieces, part):
    n = len(pieces)
    ordered = jnp.stack([pieces[(-j) % n] for j in range(n)], 0)
    return jnp.roll(ordered, part, axis=0)


def tiles_to_heads(tile, width):
    n = lax.axis_size("tp")
    part = lax.axis_index("tp")
    if NG_MODE == "a2a":
        return lax.all_to_all(tile, "tp", split_axis=1, concat_axis=0, tiled=True)
    pieces = []
    for shift in range(n):
        dest = (part + shift) % n
        chunk = lax.dynamic_slice_in_dim(tile, dest * width, width, 1)
        if shift:
            chunk = lax.ppermute(chunk, "tp", [(i, (i + shift) % n) for i in range(n)])
        pieces.append(chunk)
    return rolled(pieces, part).reshape(n * tile.shape[0], width)


def heads_to_tiles(block, rows):
    n = lax.axis_size("tp")
    part = lax.axis_index("tp")
    if OUT_MODE == "a2a":
        return lax.all_to_all(block, "tp", split_axis=0, concat_axis=1, tiled=True)
    pieces = []
    for shift in range(n):
        dest = (part + shift) % n
        chunk = lax.dynamic_slice_in_dim(block, dest * rows, rows, 0)
        if shift:
            chunk = lax.ppermute(chunk, "tp", [(i, (i + shift) % n) for i in range(n)])
        pieces.append(chunk)
    ordered = rolled(pieces, part)
    return jnp.moveaxis(ordered, 0, 1).reshape(rows, -1)


def per_device(queries, key_rows, value_rows, view_mask, norm_gain, normed_grad):
    length = queries.shape[0]
    width = queries.shape[1]
    features = norm_gain.shape[0]
    span_blocks = 2 * REACH - 1
    score_scale = HSZ ** (-0.5)
    position = lax.axis_index("ctx")
    part = lax.axis_index("tp")

    grad_tiles = tiles_to_heads(normed_grad, width)
    gain_local = lax.dynamic_slice_in_dim(norm_gain, part * width, width, 0)

    both = jnp.concatenate([key_rows, value_rows], axis=1)
    from_prev = passed_along(both, "ctx", 1)
    from_next = passed_along(both, "ctx", -1)
    key_ext = jnp.concatenate([from_prev[:, :width], key_rows, from_next[:, :width]], axis=0)
    value_ext = jnp.concatenate([from_prev[:, width:], value_rows, from_next[:, width:]], axis=0)

    mask_row = lax.dynamic_slice_in_dim(view_mask, position, 1, 0)[0]
    key_live = jnp.repeat(mask_row, length) > 0
    q_heads = split_heads(queries)
    k_heads = split_heads(key_ext)
    v_heads = split_heads(value_ext)
    scores = (
        jnp.einsum("thd,shd->hts", q_heads, k_heads, preferred_element_type=jnp.float32)
        * score_scale
    )
    scores = jnp.where(key_live[None, None, :], scores, NEGATIVE)
    peak = jnp.max(scores, -1, keepdims=True)
    log_total = peak + jnp.log(jnp.sum(jnp.exp(scores - peak), -1, keepdims=True))
    probs = jnp.exp(scores - log_total)
    probs_low = probs.astype(jnp.bfloat16)
    out_heads = jnp.einsum(
        "hts,shd->thd", probs_low, v_heads, preferred_element_type=jnp.float32
    ).astype(jnp.bfloat16)
    attended = out_heads.reshape(length, -1)

    values_f = attended.astype(jnp.float32)
    upstream = grad_tiles.astype(jnp.float32) * gain_local
    partial = jnp.stack(
        [jnp.sum(values_f * values_f, -1), jnp.sum(upstream * values_f, -1)], axis=-1
    )
    totals = tp_sum(partial)
    inverse = lax.rsqrt(totals[:, 0:1] / features + EPSILON)
    inner_mean = totals[:, 1:2] / features
    normed_heads = (values_f * inverse * gain_local).astype(jnp.bfloat16)
    normed = heads_to_tiles(normed_heads, normed_grad.shape[0])
    attended_grad = (
        inverse * upstream - values_f * inverse * inverse * inverse * inner_mean
    ).astype(jnp.bfloat16)

    grad_heads = split_heads(attended_grad)
    delta = jnp.sum(grad_heads.astype(jnp.float32) * out_heads.astype(jnp.float32), -1)
    prob_grad = jnp.einsum("thd,shd->hts", grad_heads, v_heads, preferred_element_type=jnp.float32)
    score_grad = (probs * (prob_grad - delta.T[:, :, None])).astype(jnp.bfloat16)
    query_grad = (
        (
            jnp.einsum("hts,shd->thd", score_grad, k_heads, preferred_element_type=jnp.float32)
            * score_scale
        )
        .astype(jnp.bfloat16)
        .reshape(length, -1)
    )
    key_terms = (
        jnp.einsum("hts,thd->shd", score_grad, q_heads, preferred_element_type=jnp.float32)
        * score_scale
    ).reshape(span_blocks * length, -1)
    value_terms = jnp.einsum(
        "hts,thd->shd", probs_low, grad_heads, preferred_element_type=jnp.float32
    ).reshape(span_blocks * length, -1)
    terms = jnp.concatenate([key_terms, value_terms], axis=1)
    total = terms[length : 2 * length]
    to_prev = terms[:length].astype(jnp.bfloat16)
    to_next = terms[2 * length :].astype(jnp.bfloat16)
    total = total + passed_along(to_prev, "ctx", -1).astype(jnp.float32)
    total = total + passed_along(to_next, "ctx", 1).astype(jnp.float32)
    total = total.astype(jnp.bfloat16)
    return (normed, query_grad, total[:, :width], total[:, width:])


def solution(mesh):
    placed = (P("ctx", "tp"), P("ctx", "tp"), P("ctx", "tp"), P(), P(), P(("ctx", "tp"), None))
    return jax.shard_map(
        per_device,
        mesh=mesh,
        in_specs=placed,
        out_specs=(P(("ctx", "tp"), None), P("ctx", "tp"), P("ctx", "tp"), P("ctx", "tp")),
        check_vma=False,
    )
```

```python
import jax
import jax.numpy as jnp
from jax import lax
from jax.sharding import PartitionSpec as P

HSZ = 128
REACH = 2


NEGATIVE = -1e30
EPSILON = 1e-06
STATS_SUM = "xor"
NG_MODE = "perm"
OUT_MODE = "perm"


def passed_along(x, axis, by):
    peers = lax.axis_size(axis)
    pairs = [(i, i + by) for i in range(peers) if 0 <= i + by < peers]
    return lax.ppermute(x, axis, pairs)


def split_heads(values):
    return values.reshape(values.shape[0], -1, HSZ)


def xor_flip(stacked, part, n):
    bits = n.bit_length() - 1
    view = stacked.reshape((2,) * bits + stacked.shape[1:])
    for b in range(bits):
        axis = bits - 1 - b
        view = jnp.where((part >> b) & 1 == 1, jnp.flip(view, axis), view)
    return view.reshape(stacked.shape)


def xor_exchange(stacked, n):
    bits = n.bit_length() - 1
    view = stacked.reshape((2,) * bits + stacked.shape[1:])
    for b in range(bits):
        axis = bits - 1 - b
        keep = lax.index_in_dim(view, 0, axis, keepdims=True)
        sent = lax.index_in_dim(view, 1, axis, keepdims=True)
        got = lax.ppermute(sent, "tp", [(i, i ^ (1 << b)) for i in range(n)])
        view = jnp.concatenate([keep, got], axis)
    return view.reshape(stacked.shape)


def power_of_two(n):
    return n & (n - 1) == 0


def tp_sum(stats):
    if STATS_SUM == "psum":
        return lax.psum(stats, "tp")
    peers = lax.axis_size("tp")
    if STATS_SUM == "xor" and power_of_two(peers):
        total = stats
        for b in range(peers.bit_length() - 1):
            total = total + lax.ppermute(total, "tp", [(i, i ^ (1 << b)) for i in range(peers)])
        return total
    if STATS_SUM == "a2a":
        spread = jnp.broadcast_to(stats[None], (peers,) + stats.shape)
        gathered = lax.all_to_all(spread, "tp", split_axis=0, concat_axis=0, tiled=True)
        return jnp.sum(gathered, 0)
    total = stats
    for shift in range(1, peers):
        total = total + lax.ppermute(stats, "tp", [(i, (i + shift) % peers) for i in range(peers)])
    return total


def rolled(pieces, part):
    n = len(pieces)
    ordered = jnp.stack([pieces[(-j) % n] for j in range(n)], 0)
    return jnp.roll(ordered, part, axis=0)


def tiles_to_heads(tile, width):
    n = lax.axis_size("tp")
    part = lax.axis_index("tp")
    if NG_MODE == "a2a":
        return lax.all_to_all(tile, "tp", split_axis=1, concat_axis=0, tiled=True)
    if NG_MODE == "xor" and power_of_two(n):
        groups = jnp.moveaxis(tile.reshape(tile.shape[0], n, width), 1, 0)
        got = xor_flip(xor_exchange(xor_flip(groups, part, n), n), part, n)
        return got.reshape(n * tile.shape[0], width)
    pieces = []
    for shift in range(n):
        dest = (part + shift) % n
        chunk = lax.dynamic_slice_in_dim(tile, dest * width, width, 1)
        if shift:
            chunk = lax.ppermute(chunk, "tp", [(i, (i + shift) % n) for i in range(n)])
        pieces.append(chunk)
    return rolled(pieces, part).reshape(n * tile.shape[0], width)


def heads_to_tiles(block, rows):
    n = lax.axis_size("tp")
    part = lax.axis_index("tp")
    if OUT_MODE == "a2a":
        return lax.all_to_all(block, "tp", split_axis=0, concat_axis=1, tiled=True)
    if OUT_MODE == "xor" and power_of_two(n):
        tiles = block.reshape(n, rows, block.shape[1])
        got = xor_flip(xor_exchange(xor_flip(tiles, part, n), n), part, n)
        return jnp.moveaxis(got, 0, 1).reshape(rows, -1)
    pieces = []
    for shift in range(n):
        dest = (part + shift) % n
        chunk = lax.dynamic_slice_in_dim(block, dest * rows, rows, 0)
        if shift:
            chunk = lax.ppermute(chunk, "tp", [(i, (i + shift) % n) for i in range(n)])
        pieces.append(chunk)
    ordered = rolled(pieces, part)
    return jnp.moveaxis(ordered, 0, 1).reshape(rows, -1)


def per_device(queries, key_rows, value_rows, view_mask, norm_gain, normed_grad):
    length = queries.shape[0]
    width = queries.shape[1]
    features = norm_gain.shape[0]
    span_blocks = 2 * REACH - 1
    score_scale = HSZ ** (-0.5)
    position = lax.axis_index("ctx")
    part = lax.axis_index("tp")

    grad_tiles = tiles_to_heads(normed_grad, width)
    gain_local = lax.dynamic_slice_in_dim(norm_gain, part * width, width, 0)

    both = jnp.concatenate([key_rows, value_rows], axis=1)
    from_prev = passed_along(both, "ctx", 1)
    from_next = passed_along(both, "ctx", -1)
    key_ext = jnp.concatenate([from_prev[:, :width], key_rows, from_next[:, :width]], axis=0)
    value_ext = jnp.concatenate([from_prev[:, width:], value_rows, from_next[:, width:]], axis=0)

    mask_row = lax.dynamic_slice_in_dim(view_mask, position, 1, 0)[0]
    key_live = jnp.repeat(mask_row, length) > 0
    q_heads = split_heads(queries)
    k_heads = split_heads(key_ext)
    v_heads = split_heads(value_ext)
    scores = (
        jnp.einsum("thd,shd->hts", q_heads, k_heads, preferred_element_type=jnp.float32)
        * score_scale
    )
    scores = jnp.where(key_live[None, None, :], scores, NEGATIVE)
    peak = jnp.max(scores, -1, keepdims=True)
    log_total = peak + jnp.log(jnp.sum(jnp.exp(scores - peak), -1, keepdims=True))
    probs = jnp.exp(scores - log_total)
    probs_low = probs.astype(jnp.bfloat16)
    out_heads = jnp.einsum(
        "hts,shd->thd", probs_low, v_heads, preferred_element_type=jnp.float32
    ).astype(jnp.bfloat16)
    attended = out_heads.reshape(length, -1)

    values_f = attended.astype(jnp.float32)
    upstream = grad_tiles.astype(jnp.float32) * gain_local
    partial = jnp.stack(
        [jnp.sum(values_f * values_f, -1), jnp.sum(upstream * values_f, -1)], axis=-1
    )
    totals = tp_sum(partial)
    inverse = lax.rsqrt(totals[:, 0:1] / features + EPSILON)
    inner_mean = totals[:, 1:2] / features
    normed_heads = (values_f * inverse * gain_local).astype(jnp.bfloat16)
    normed = heads_to_tiles(normed_heads, normed_grad.shape[0])
    attended_grad = (
        inverse * upstream - values_f * inverse * inverse * inverse * inner_mean
    ).astype(jnp.bfloat16)

    grad_heads = split_heads(attended_grad)
    delta = jnp.sum(grad_heads.astype(jnp.float32) * out_heads.astype(jnp.float32), -1)
    prob_grad = jnp.einsum("thd,shd->hts", grad_heads, v_heads, preferred_element_type=jnp.float32)
    score_grad = (probs * (prob_grad - delta.T[:, :, None])).astype(jnp.bfloat16)
    query_grad = (
        (
            jnp.einsum("hts,shd->thd", score_grad, k_heads, preferred_element_type=jnp.float32)
            * score_scale
        )
        .astype(jnp.bfloat16)
        .reshape(length, -1)
    )
    key_terms = (
        jnp.einsum("hts,thd->shd", score_grad, q_heads, preferred_element_type=jnp.float32)
        * score_scale
    ).reshape(span_blocks * length, -1)
    value_terms = jnp.einsum(
        "hts,thd->shd", probs_low, grad_heads, preferred_element_type=jnp.float32
    ).reshape(span_blocks * length, -1)
    terms = jnp.concatenate([key_terms, value_terms], axis=1)
    total = terms[length : 2 * length]
    to_prev = terms[:length].astype(jnp.bfloat16)
    to_next = terms[2 * length :].astype(jnp.bfloat16)
    total = total + passed_along(to_prev, "ctx", -1).astype(jnp.float32)
    total = total + passed_along(to_next, "ctx", 1).astype(jnp.float32)
    total = total.astype(jnp.bfloat16)
    return (normed, query_grad, total[:, :width], total[:, width:])


def solution(mesh):
    placed = (P("ctx", "tp"), P("ctx", "tp"), P("ctx", "tp"), P(), P(), P(("ctx", "tp"), None))
    return jax.shard_map(
        per_device,
        mesh=mesh,
        in_specs=placed,
        out_specs=(P(("ctx", "tp"), None), P("ctx", "tp"), P("ctx", "tp"), P("ctx", "tp")),
        check_vma=False,
    )
```

```python
import functools

import jax
import jax.numpy as jnp
from jax import lax
from jax.experimental import pallas as pl
from jax.experimental.pallas import tpu as pltpu
from jax.sharding import PartitionSpec as P

HSZ = 128
REACH = 2


NEGATIVE = -1e30
EPSILON = 1e-06
STATS_SUM = "xor"
NG_MODE = "perm"
OUT_MODE = "perm"


def passed_along(x, axis, by):
    peers = lax.axis_size(axis)
    pairs = [(i, i + by) for i in range(peers) if 0 <= i + by < peers]
    return lax.ppermute(x, axis, pairs)


def split_heads(values):
    return values.reshape(values.shape[0], -1, HSZ)


def xor_flip(stacked, part, n):
    bits = n.bit_length() - 1
    view = stacked.reshape((2,) * bits + stacked.shape[1:])
    for b in range(bits):
        axis = bits - 1 - b
        view = jnp.where((part >> b) & 1 == 1, jnp.flip(view, axis), view)
    return view.reshape(stacked.shape)


def xor_exchange(stacked, n):
    bits = n.bit_length() - 1
    view = stacked.reshape((2,) * bits + stacked.shape[1:])
    for b in range(bits):
        axis = bits - 1 - b
        keep = lax.index_in_dim(view, 0, axis, keepdims=True)
        sent = lax.index_in_dim(view, 1, axis, keepdims=True)
        got = lax.ppermute(sent, "tp", [(i, i ^ (1 << b)) for i in range(n)])
        view = jnp.concatenate([keep, got], axis)
    return view.reshape(stacked.shape)


def power_of_two(n):
    return n & (n - 1) == 0


def tp_sum(stats):
    if STATS_SUM == "psum":
        return lax.psum(stats, "tp")
    peers = lax.axis_size("tp")
    if STATS_SUM == "xor" and power_of_two(peers):
        total = stats
        for b in range(peers.bit_length() - 1):
            total = total + lax.ppermute(total, "tp", [(i, i ^ (1 << b)) for i in range(peers)])
        return total
    if STATS_SUM == "a2a":
        spread = jnp.broadcast_to(stats[None], (peers,) + stats.shape)
        gathered = lax.all_to_all(spread, "tp", split_axis=0, concat_axis=0, tiled=True)
        return jnp.sum(gathered, 0)
    total = stats
    for shift in range(1, peers):
        total = total + lax.ppermute(stats, "tp", [(i, (i + shift) % peers) for i in range(peers)])
    return total


def rolled(pieces, part):
    n = len(pieces)
    ordered = jnp.stack([pieces[(-j) % n] for j in range(n)], 0)
    return jnp.roll(ordered, part, axis=0)


def tiles_to_heads(tile, width):
    n = lax.axis_size("tp")
    part = lax.axis_index("tp")
    if NG_MODE == "a2a":
        return lax.all_to_all(tile, "tp", split_axis=1, concat_axis=0, tiled=True)
    if NG_MODE == "xor" and power_of_two(n):
        groups = jnp.moveaxis(tile.reshape(tile.shape[0], n, width), 1, 0)
        got = xor_flip(xor_exchange(xor_flip(groups, part, n), n), part, n)
        return got.reshape(n * tile.shape[0], width)
    pieces = []
    for shift in range(n):
        dest = (part + shift) % n
        chunk = lax.dynamic_slice_in_dim(tile, dest * width, width, 1)
        if shift:
            chunk = lax.ppermute(chunk, "tp", [(i, (i + shift) % n) for i in range(n)])
        pieces.append(chunk)
    return rolled(pieces, part).reshape(n * tile.shape[0], width)


def heads_to_tiles(block, rows):
    n = lax.axis_size("tp")
    part = lax.axis_index("tp")
    if OUT_MODE == "a2a":
        return lax.all_to_all(block, "tp", split_axis=0, concat_axis=1, tiled=True)
    if OUT_MODE == "xor" and power_of_two(n):
        tiles = block.reshape(n, rows, block.shape[1])
        got = xor_flip(xor_exchange(xor_flip(tiles, part, n), n), part, n)
        return jnp.moveaxis(got, 0, 1).reshape(rows, -1)
    pieces = []
    for shift in range(n):
        dest = (part + shift) % n
        chunk = lax.dynamic_slice_in_dim(block, dest * rows, rows, 0)
        if shift:
            chunk = lax.ppermute(chunk, "tp", [(i, (i + shift) % n) for i in range(n)])
        pieces.append(chunk)
    ordered = rolled(pieces, part)
    return jnp.moveaxis(ordered, 0, 1).reshape(rows, -1)


def _nt(a, b):
    return lax.dot_general(a, b, (((1,), (1,)), ((), ())), preferred_element_type=jnp.float32)


def _nn(a, b):
    return lax.dot_general(a, b, (((1,), (0,)), ((), ())), preferred_element_type=jnp.float32)


def _tn(a, b):
    return lax.dot_general(a, b, (((0,), (0,)), ((), ())), preferred_element_type=jnp.float32)


def _scores(mask_ref, q, keys, scale):
    parts = []
    for c, k in enumerate(keys):
        s = _nt(q, k) * scale
        parts.append(jnp.where(mask_ref[c] > 0, s, NEGATIVE))
    return jnp.concatenate(parts, axis=1)


def _window(k_ref, v_ref, prev_ref, next_ref, h):
    width = k_ref.shape[1]
    cols = slice(h * HSZ, (h + 1) * HSZ)
    far = slice(width + h * HSZ, width + (h + 1) * HSZ)
    keys = [prev_ref[:, cols], k_ref[:, cols], next_ref[:, cols]]
    values = [prev_ref[:, far], v_ref[:, cols], next_ref[:, far]]
    return keys, values


def _forward_kernel(mask_ref, q_ref, k_ref, v_ref, prev_ref, next_ref, out_ref, lse_ref, *, heads, scale):
    for h in range(heads):
        cols = slice(h * HSZ, (h + 1) * HSZ)
        q = q_ref[:, cols]
        keys, values = _window(k_ref, v_ref, prev_ref, next_ref, h)
        s = _scores(mask_ref, q, keys, scale)
        peak = jnp.max(s, -1, keepdims=True)
        lse = peak + jnp.log(jnp.sum(jnp.exp(s - peak), -1, keepdims=True))
        p = jnp.exp(s - lse).astype(jnp.bfloat16)
        v = jnp.concatenate(values, axis=0)
        out_ref[:, cols] = _nn(p, v).astype(out_ref.dtype)
        lse_ref[:, h:h + 1] = lse


def attend_forward(mask_row, q, k, v, kv_prev, kv_next):
    length, width = q.shape
    heads = width // HSZ
    kern = functools.partial(_forward_kernel, heads=heads, scale=HSZ ** (-0.5))
    vmem = pl.BlockSpec(memory_space=pltpu.VMEM)
    return pl.pallas_call(
        kern,
        out_shape=(jax.ShapeDtypeStruct((length, width), jnp.bfloat16),
                   jax.ShapeDtypeStruct((length, heads), jnp.float32)),
        in_specs=[pl.BlockSpec(memory_space=pltpu.SMEM)] + [vmem] * 5,
        out_specs=(vmem, vmem),
        cost_estimate=pl.CostEstimate(
            flops=12 * length * length * width, transcendentals=6 * length * length * heads,
            bytes_accessed=16 * length * width),
    )(mask_row, q, k, v, kv_prev, kv_next)


def _backward_kernel(mask_ref, q_ref, k_ref, v_ref, kvp_ref, kvn_ref, g_ref, lse_ref, delta_ref,
                     dq_ref, prev_ref, next_ref, own_ref, *, heads, scale):
    length = q_ref.shape[0]
    width = q_ref.shape[1]
    for h in range(heads):
        cols = slice(h * HSZ, (h + 1) * HSZ)
        q = q_ref[:, cols]
        g = g_ref[:, cols]
        keys, vals = _window(k_ref, v_ref, kvp_ref, kvn_ref, h)
        s = _scores(mask_ref, q, keys, scale)
        p = jnp.exp(s - lse_ref[:, h:h + 1])
        dp = jnp.concatenate([_nt(g, v) for v in vals], axis=1)
        ds = (p * (dp - delta_ref[:, h:h + 1])).astype(jnp.bfloat16)
        p_low = p.astype(jnp.bfloat16)
        dq_ref[:, cols] = (_nn(ds, jnp.concatenate(keys, axis=0)) * scale).astype(dq_ref.dtype)
        for c, ref in enumerate((prev_ref, own_ref, next_ref)):
            blk = slice(c * length, (c + 1) * length)
            dk = _tn(ds[:, blk], q) * scale
            dv = _tn(p_low[:, blk], g)
            ref[:, cols] = dk.astype(ref.dtype)
            ref[:, width + h * HSZ:width + (h + 1) * HSZ] = dv.astype(ref.dtype)


def attend_backward(mask_row, q, k, v, kv_prev, kv_next, grad, lse, delta):
    length, width = q.shape
    heads = width // HSZ
    kern = functools.partial(_backward_kernel, heads=heads, scale=HSZ ** (-0.5))
    vmem = pl.BlockSpec(memory_space=pltpu.VMEM)
    sent = jax.ShapeDtypeStruct((length, 2 * width), jnp.bfloat16)
    return pl.pallas_call(
        kern,
        out_shape=(jax.ShapeDtypeStruct((length, width), jnp.bfloat16), sent, sent,
                   jax.ShapeDtypeStruct((length, 2 * width), jnp.float32)),
        in_specs=[pl.BlockSpec(memory_space=pltpu.SMEM)] + [vmem] * 8,
        out_specs=(vmem, vmem, vmem, vmem),
        cost_estimate=pl.CostEstimate(
            flops=30 * length * length * width, transcendentals=3 * length * length * heads,
            bytes_accessed=36 * length * width),
    )(mask_row, q, k, v, kv_prev, kv_next, grad, lse, delta)


def per_device(queries, key_rows, value_rows, view_mask, norm_gain, normed_grad):
    length = queries.shape[0]
    width = queries.shape[1]
    features = norm_gain.shape[0]
    position = lax.axis_index("ctx")
    part = lax.axis_index("tp")

    grad_tiles = tiles_to_heads(normed_grad, width)
    gain_local = lax.dynamic_slice_in_dim(norm_gain, part * width, width, 0)

    both = jnp.concatenate([key_rows, value_rows], axis=1)
    from_prev = passed_along(both, "ctx", 1)
    from_next = passed_along(both, "ctx", -1)
    mask_row = lax.dynamic_slice_in_dim(view_mask, position, 1, 0)[0]
    attended, log_total = attend_forward(mask_row, queries, key_rows, value_rows, from_prev, from_next)
    out_heads = split_heads(attended)

    values_f = attended.astype(jnp.float32)
    upstream = grad_tiles.astype(jnp.float32) * gain_local
    partial = jnp.stack(
        [jnp.sum(values_f * values_f, -1), jnp.sum(upstream * values_f, -1)], axis=-1
    )
    totals = tp_sum(partial)
    inverse = lax.rsqrt(totals[:, 0:1] / features + EPSILON)
    inner_mean = totals[:, 1:2] / features
    normed_heads = (values_f * inverse * gain_local).astype(jnp.bfloat16)
    normed = heads_to_tiles(normed_heads, normed_grad.shape[0])
    attended_grad = (
        inverse * upstream - values_f * inverse * inverse * inverse * inner_mean
    ).astype(jnp.bfloat16)

    grad_heads = split_heads(attended_grad)
    delta = jnp.sum(grad_heads.astype(jnp.float32) * out_heads.astype(jnp.float32), -1)
    query_grad, to_prev, to_next, own = attend_backward(
        mask_row, queries, key_rows, value_rows, from_prev, from_next, attended_grad, log_total, delta)
    total = own + passed_along(to_prev, "ctx", -1).astype(jnp.float32)
    total = total + passed_along(to_next, "ctx", 1).astype(jnp.float32)
    total = total.astype(jnp.bfloat16)
    return (normed, query_grad, total[:, :width], total[:, width:])

def solution(mesh):
    placed = (P("ctx", "tp"), P("ctx", "tp"), P("ctx", "tp"), P(), P(), P(("ctx", "tp"), None))
    return jax.shard_map(
        per_device,
        mesh=mesh,
        in_specs=placed,
        out_specs=(P(("ctx", "tp"), None), P("ctx", "tp"), P("ctx", "tp"), P("ctx", "tp")),
        check_vma=False,
    )
```

```python
import functools

import jax
import jax.numpy as jnp
from jax import lax
from jax.experimental import pallas as pl
from jax.experimental.pallas import tpu as pltpu
from jax.sharding import PartitionSpec as P

HSZ = 128
REACH = 2


NEGATIVE = -1e30
EPSILON = 1e-06
STATS_SUM = "xor"
NG_MODE = "perm"
OUT_MODE = "perm"


def passed_along(x, axis, by):
    peers = lax.axis_size(axis)
    pairs = [(i, i + by) for i in range(peers) if 0 <= i + by < peers]
    return lax.ppermute(x, axis, pairs)


def split_heads(values):
    return values.reshape(values.shape[0], -1, HSZ)


def xor_flip(stacked, part, n):
    bits = n.bit_length() - 1
    view = stacked.reshape((2,) * bits + stacked.shape[1:])
    for b in range(bits):
        axis = bits - 1 - b
        view = jnp.where((part >> b) & 1 == 1, jnp.flip(view, axis), view)
    return view.reshape(stacked.shape)


def xor_exchange(stacked, n):
    bits = n.bit_length() - 1
    view = stacked.reshape((2,) * bits + stacked.shape[1:])
    for b in range(bits):
        axis = bits - 1 - b
        keep = lax.index_in_dim(view, 0, axis, keepdims=True)
        sent = lax.index_in_dim(view, 1, axis, keepdims=True)
        got = lax.ppermute(sent, "tp", [(i, i ^ (1 << b)) for i in range(n)])
        view = jnp.concatenate([keep, got], axis)
    return view.reshape(stacked.shape)


def power_of_two(n):
    return n & (n - 1) == 0


def tp_sum(stats):
    if STATS_SUM == "psum":
        return lax.psum(stats, "tp")
    peers = lax.axis_size("tp")
    if STATS_SUM == "xor" and power_of_two(peers):
        total = stats
        for b in range(peers.bit_length() - 1):
            total = total + lax.ppermute(total, "tp", [(i, i ^ (1 << b)) for i in range(peers)])
        return total
    if STATS_SUM == "a2a":
        spread = jnp.broadcast_to(stats[None], (peers,) + stats.shape)
        gathered = lax.all_to_all(spread, "tp", split_axis=0, concat_axis=0, tiled=True)
        return jnp.sum(gathered, 0)
    total = stats
    for shift in range(1, peers):
        total = total + lax.ppermute(stats, "tp", [(i, (i + shift) % peers) for i in range(peers)])
    return total


def rolled(pieces, part):
    n = len(pieces)
    ordered = jnp.stack([pieces[(-j) % n] for j in range(n)], 0)
    return jnp.roll(ordered, part, axis=0)


def tiles_to_heads(tile, width):
    n = lax.axis_size("tp")
    part = lax.axis_index("tp")
    if NG_MODE == "a2a":
        return lax.all_to_all(tile, "tp", split_axis=1, concat_axis=0, tiled=True)
    if NG_MODE == "xor" and power_of_two(n):
        groups = jnp.moveaxis(tile.reshape(tile.shape[0], n, width), 1, 0)
        got = xor_flip(xor_exchange(xor_flip(groups, part, n), n), part, n)
        return got.reshape(n * tile.shape[0], width)
    pieces = []
    for shift in range(n):
        dest = (part + shift) % n
        chunk = lax.dynamic_slice_in_dim(tile, dest * width, width, 1)
        if shift:
            chunk = lax.ppermute(chunk, "tp", [(i, (i + shift) % n) for i in range(n)])
        pieces.append(chunk)
    return rolled(pieces, part).reshape(n * tile.shape[0], width)


def heads_to_tiles(block, rows):
    n = lax.axis_size("tp")
    part = lax.axis_index("tp")
    if OUT_MODE == "a2a":
        return lax.all_to_all(block, "tp", split_axis=0, concat_axis=1, tiled=True)
    if OUT_MODE == "xor" and power_of_two(n):
        tiles = block.reshape(n, rows, block.shape[1])
        got = xor_flip(xor_exchange(xor_flip(tiles, part, n), n), part, n)
        return jnp.moveaxis(got, 0, 1).reshape(rows, -1)
    pieces = []
    for shift in range(n):
        dest = (part + shift) % n
        chunk = lax.dynamic_slice_in_dim(block, dest * rows, rows, 0)
        if shift:
            chunk = lax.ppermute(chunk, "tp", [(i, (i + shift) % n) for i in range(n)])
        pieces.append(chunk)
    ordered = rolled(pieces, part)
    return jnp.moveaxis(ordered, 0, 1).reshape(rows, -1)


def _nt(a, b):
    return lax.dot_general(a, b, (((1,), (1,)), ((), ())), preferred_element_type=jnp.float32)


def _nn(a, b):
    return lax.dot_general(a, b, (((1,), (0,)), ((), ())), preferred_element_type=jnp.float32)


def _tn(a, b):
    return lax.dot_general(a, b, (((0,), (0,)), ((), ())), preferred_element_type=jnp.float32)


def _scores(mask_ref, q, keys, scale):
    parts = []
    for c, k in enumerate(keys):
        s = _nt(q, k) * scale
        parts.append(jnp.where(mask_ref[c] > 0, s, NEGATIVE))
    return jnp.concatenate(parts, axis=1)


def _window(k_ref, v_ref, prev_ref, next_ref, h):
    width = k_ref.shape[1]
    cols = slice(h * HSZ, (h + 1) * HSZ)
    far = slice(width + h * HSZ, width + (h + 1) * HSZ)
    keys = [prev_ref[:, cols], k_ref[:, cols], next_ref[:, cols]]
    values = [prev_ref[:, far], v_ref[:, cols], next_ref[:, far]]
    return keys, values


def _forward_kernel(mask_ref, q_ref, k_ref, v_ref, prev_ref, next_ref, out_ref, lse_ref, *, heads, scale):
    def scores(h):
        keys, values = _window(k_ref, v_ref, prev_ref, next_ref, h)
        return _scores(mask_ref, q_ref[:, h * HSZ:(h + 1) * HSZ], keys, scale), values

    ahead = scores(0)
    for h in range(heads):
        s, values = ahead
        if h + 1 < heads:
            ahead = scores(h + 1)
        peak = jnp.max(s, -1, keepdims=True)
        lse = peak + jnp.log(jnp.sum(jnp.exp(s - peak), -1, keepdims=True))
        p = jnp.exp(s - lse).astype(jnp.bfloat16)
        v = jnp.concatenate(values, axis=0)
        out_ref[:, h * HSZ:(h + 1) * HSZ] = _nn(p, v).astype(out_ref.dtype)
        lse_ref[:, h:h + 1] = lse


def attend_forward(mask_row, q, k, v, kv_prev, kv_next):
    length, width = q.shape
    heads = width // HSZ
    kern = functools.partial(_forward_kernel, heads=heads, scale=HSZ ** (-0.5))
    vmem = pl.BlockSpec(memory_space=pltpu.VMEM)
    return pl.pallas_call(
        kern,
        out_shape=(jax.ShapeDtypeStruct((length, width), jnp.bfloat16),
                   jax.ShapeDtypeStruct((length, heads), jnp.float32)),
        in_specs=[pl.BlockSpec(memory_space=pltpu.SMEM)] + [vmem] * 5,
        out_specs=(vmem, vmem),
        cost_estimate=pl.CostEstimate(
            flops=12 * length * length * width, transcendentals=6 * length * length * heads,
            bytes_accessed=16 * length * width),
    )(mask_row, q, k, v, kv_prev, kv_next)


def _backward_kernel(mask_ref, q_ref, k_ref, v_ref, kvp_ref, kvn_ref, g_ref, lse_ref, delta_ref,
                     dq_ref, prev_ref, next_ref, own_ref, *, heads, scale):
    length = q_ref.shape[0]
    width = q_ref.shape[1]

    def front(h):
        cols = slice(h * HSZ, (h + 1) * HSZ)
        q = q_ref[:, cols]
        g = g_ref[:, cols]
        keys, vals = _window(k_ref, v_ref, kvp_ref, kvn_ref, h)
        s = _scores(mask_ref, q, keys, scale)
        dp = jnp.concatenate([_nt(g, v) for v in vals], axis=1)
        return q, g, keys, s, dp

    ahead = front(0)
    for h in range(heads):
        cols = slice(h * HSZ, (h + 1) * HSZ)
        q, g, keys, s, dp = ahead
        if h + 1 < heads:
            ahead = front(h + 1)
        p = jnp.exp(s - lse_ref[:, h:h + 1])
        ds = (p * (dp - delta_ref[:, h:h + 1])).astype(jnp.bfloat16)
        p_low = p.astype(jnp.bfloat16)
        dq_ref[:, cols] = (_nn(ds, jnp.concatenate(keys, axis=0)) * scale).astype(dq_ref.dtype)
        for c, ref in enumerate((prev_ref, own_ref, next_ref)):
            blk = slice(c * length, (c + 1) * length)
            dk = _tn(ds[:, blk], q) * scale
            dv = _tn(p_low[:, blk], g)
            ref[:, cols] = dk.astype(ref.dtype)
            ref[:, width + h * HSZ:width + (h + 1) * HSZ] = dv.astype(ref.dtype)


def attend_backward(mask_row, q, k, v, kv_prev, kv_next, grad, lse, delta):
    length, width = q.shape
    heads = width // HSZ
    kern = functools.partial(_backward_kernel, heads=heads, scale=HSZ ** (-0.5))
    vmem = pl.BlockSpec(memory_space=pltpu.VMEM)
    sent = jax.ShapeDtypeStruct((length, 2 * width), jnp.bfloat16)
    return pl.pallas_call(
        kern,
        out_shape=(jax.ShapeDtypeStruct((length, width), jnp.bfloat16), sent, sent,
                   jax.ShapeDtypeStruct((length, 2 * width), jnp.float32)),
        in_specs=[pl.BlockSpec(memory_space=pltpu.SMEM)] + [vmem] * 8,
        out_specs=(vmem, vmem, vmem, vmem),
        cost_estimate=pl.CostEstimate(
            flops=30 * length * length * width, transcendentals=3 * length * length * heads,
            bytes_accessed=36 * length * width),
    )(mask_row, q, k, v, kv_prev, kv_next, grad, lse, delta)


def per_device(queries, key_rows, value_rows, view_mask, norm_gain, normed_grad):
    length = queries.shape[0]
    width = queries.shape[1]
    features = norm_gain.shape[0]
    position = lax.axis_index("ctx")
    part = lax.axis_index("tp")

    grad_tiles = tiles_to_heads(normed_grad, width)
    gain_local = lax.dynamic_slice_in_dim(norm_gain, part * width, width, 0)

    both = jnp.concatenate([key_rows, value_rows], axis=1)
    from_prev = passed_along(both, "ctx", 1)
    from_next = passed_along(both, "ctx", -1)
    mask_row = lax.dynamic_slice_in_dim(view_mask, position, 1, 0)[0]
    attended, log_total = attend_forward(mask_row, queries, key_rows, value_rows, from_prev, from_next)
    out_heads = split_heads(attended)

    values_f = attended.astype(jnp.float32)
    upstream = grad_tiles.astype(jnp.float32) * gain_local
    partial = jnp.stack(
        [jnp.sum(values_f * values_f, -1), jnp.sum(upstream * values_f, -1)], axis=-1
    )
    totals = tp_sum(partial)
    inverse = lax.rsqrt(totals[:, 0:1] / features + EPSILON)
    inner_mean = totals[:, 1:2] / features
    normed_heads = (values_f * inverse * gain_local).astype(jnp.bfloat16)
    normed = heads_to_tiles(normed_heads, normed_grad.shape[0])
    attended_grad = (
        inverse * upstream - values_f * inverse * inverse * inverse * inner_mean
    ).astype(jnp.bfloat16)

    grad_heads = split_heads(attended_grad)
    delta = jnp.sum(grad_heads.astype(jnp.float32) * out_heads.astype(jnp.float32), -1)
    query_grad, to_prev, to_next, own = attend_backward(
        mask_row, queries, key_rows, value_rows, from_prev, from_next, attended_grad, log_total, delta)
    total = own + passed_along(to_prev, "ctx", -1).astype(jnp.float32)
    total = total + passed_along(to_next, "ctx", 1).astype(jnp.float32)
    total = total.astype(jnp.bfloat16)
    return (normed, query_grad, total[:, :width], total[:, width:])

def solution(mesh):
    placed = (P("ctx", "tp"), P("ctx", "tp"), P("ctx", "tp"), P(), P(), P(("ctx", "tp"), None))
    return jax.shard_map(
        per_device,
        mesh=mesh,
        in_specs=placed,
        out_specs=(P(("ctx", "tp"), None), P("ctx", "tp"), P("ctx", "tp"), P("ctx", "tp")),
        check_vma=False,
    )
```

```python
import functools

import jax
import jax.numpy as jnp
from jax import lax
from jax.experimental import pallas as pl
from jax.experimental.pallas import tpu as pltpu
from jax.sharding import PartitionSpec as P

HSZ = 128
REACH = 2


NEGATIVE = -1e30
EPSILON = 1e-06
LOOKAHEAD = 3
STATS_SUM = "xor"
NG_MODE = "perm"
OUT_MODE = "perm"


def passed_along(x, axis, by):
    peers = lax.axis_size(axis)
    pairs = [(i, i + by) for i in range(peers) if 0 <= i + by < peers]
    return lax.ppermute(x, axis, pairs)


def split_heads(values):
    return values.reshape(values.shape[0], -1, HSZ)


def xor_flip(stacked, part, n):
    bits = n.bit_length() - 1
    view = stacked.reshape((2,) * bits + stacked.shape[1:])
    for b in range(bits):
        axis = bits - 1 - b
        view = jnp.where((part >> b) & 1 == 1, jnp.flip(view, axis), view)
    return view.reshape(stacked.shape)


def xor_exchange(stacked, n):
    bits = n.bit_length() - 1
    view = stacked.reshape((2,) * bits + stacked.shape[1:])
    for b in range(bits):
        axis = bits - 1 - b
        keep = lax.index_in_dim(view, 0, axis, keepdims=True)
        sent = lax.index_in_dim(view, 1, axis, keepdims=True)
        got = lax.ppermute(sent, "tp", [(i, i ^ (1 << b)) for i in range(n)])
        view = jnp.concatenate([keep, got], axis)
    return view.reshape(stacked.shape)


def power_of_two(n):
    return n & (n - 1) == 0


def tp_sum(stats):
    if STATS_SUM == "psum":
        return lax.psum(stats, "tp")
    peers = lax.axis_size("tp")
    if STATS_SUM == "xor" and power_of_two(peers):
        total = stats
        for b in range(peers.bit_length() - 1):
            total = total + lax.ppermute(total, "tp", [(i, i ^ (1 << b)) for i in range(peers)])
        return total
    if STATS_SUM == "a2a":
        spread = jnp.broadcast_to(stats[None], (peers,) + stats.shape)
        gathered = lax.all_to_all(spread, "tp", split_axis=0, concat_axis=0, tiled=True)
        return jnp.sum(gathered, 0)
    total = stats
    for shift in range(1, peers):
        total = total + lax.ppermute(stats, "tp", [(i, (i + shift) % peers) for i in range(peers)])
    return total


def rolled(pieces, part):
    n = len(pieces)
    ordered = jnp.stack([pieces[(-j) % n] for j in range(n)], 0)
    return jnp.roll(ordered, part, axis=0)


def tiles_to_heads(tile, width):
    n = lax.axis_size("tp")
    part = lax.axis_index("tp")
    if NG_MODE == "a2a":
        return lax.all_to_all(tile, "tp", split_axis=1, concat_axis=0, tiled=True)
    if NG_MODE == "xor" and power_of_two(n):
        groups = jnp.moveaxis(tile.reshape(tile.shape[0], n, width), 1, 0)
        got = xor_flip(xor_exchange(xor_flip(groups, part, n), n), part, n)
        return got.reshape(n * tile.shape[0], width)
    pieces = []
    for shift in range(n):
        dest = (part + shift) % n
        chunk = lax.dynamic_slice_in_dim(tile, dest * width, width, 1)
        if shift:
            chunk = lax.ppermute(chunk, "tp", [(i, (i + shift) % n) for i in range(n)])
        pieces.append(chunk)
    return rolled(pieces, part).reshape(n * tile.shape[0], width)


def heads_to_tiles(block, rows):
    n = lax.axis_size("tp")
    part = lax.axis_index("tp")
    if OUT_MODE == "a2a":
        return lax.all_to_all(block, "tp", split_axis=0, concat_axis=1, tiled=True)
    if OUT_MODE == "xor" and power_of_two(n):
        tiles = block.reshape(n, rows, block.shape[1])
        got = xor_flip(xor_exchange(xor_flip(tiles, part, n), n), part, n)
        return jnp.moveaxis(got, 0, 1).reshape(rows, -1)
    pieces = []
    for shift in range(n):
        dest = (part + shift) % n
        chunk = lax.dynamic_slice_in_dim(block, dest * rows, rows, 0)
        if shift:
            chunk = lax.ppermute(chunk, "tp", [(i, (i + shift) % n) for i in range(n)])
        pieces.append(chunk)
    ordered = rolled(pieces, part)
    return jnp.moveaxis(ordered, 0, 1).reshape(rows, -1)


def _nt(a, b):
    return lax.dot_general(a, b, (((1,), (1,)), ((), ())), preferred_element_type=jnp.float32)


def _nn(a, b):
    return lax.dot_general(a, b, (((1,), (0,)), ((), ())), preferred_element_type=jnp.float32)


def _tn(a, b):
    return lax.dot_general(a, b, (((0,), (0,)), ((), ())), preferred_element_type=jnp.float32)


def _scores(mask_ref, q, keys, scale):
    parts = []
    for c, k in enumerate(keys):
        s = _nt(q, k) * scale
        parts.append(jnp.where(mask_ref[c] > 0, s, NEGATIVE))
    return jnp.concatenate(parts, axis=1)


def _window(k_ref, v_ref, prev_ref, next_ref, h):
    width = k_ref.shape[1]
    cols = slice(h * HSZ, (h + 1) * HSZ)
    far = slice(width + h * HSZ, width + (h + 1) * HSZ)
    keys = [prev_ref[:, cols], k_ref[:, cols], next_ref[:, cols]]
    values = [prev_ref[:, far], v_ref[:, cols], next_ref[:, far]]
    return keys, values


def _forward_kernel(mask_ref, q_ref, k_ref, v_ref, prev_ref, next_ref, out_ref, lse_ref, *, heads, scale):
    def scores(h):
        keys, values = _window(k_ref, v_ref, prev_ref, next_ref, h)
        return _scores(mask_ref, q_ref[:, h * HSZ:(h + 1) * HSZ], keys, scale), values

    ahead = [scores(h) for h in range(min(LOOKAHEAD, heads))]
    for h in range(heads):
        s, values = ahead.pop(0)
        if h + LOOKAHEAD < heads:
            ahead.append(scores(h + LOOKAHEAD))
        peak = jnp.max(s, -1, keepdims=True)
        lse = peak + jnp.log(jnp.sum(jnp.exp(s - peak), -1, keepdims=True))
        p = jnp.exp(s - lse).astype(jnp.bfloat16)
        v = jnp.concatenate(values, axis=0)
        out_ref[:, h * HSZ:(h + 1) * HSZ] = _nn(p, v).astype(out_ref.dtype)
        lse_ref[:, h:h + 1] = lse


def attend_forward(mask_row, q, k, v, kv_prev, kv_next):
    length, width = q.shape
    heads = width // HSZ
    kern = functools.partial(_forward_kernel, heads=heads, scale=HSZ ** (-0.5))
    vmem = pl.BlockSpec(memory_space=pltpu.VMEM)
    return pl.pallas_call(
        kern,
        out_shape=(jax.ShapeDtypeStruct((length, width), jnp.bfloat16),
                   jax.ShapeDtypeStruct((length, heads), jnp.float32)),
        in_specs=[pl.BlockSpec(memory_space=pltpu.SMEM)] + [vmem] * 5,
        out_specs=(vmem, vmem),
        cost_estimate=pl.CostEstimate(
            flops=12 * length * length * width, transcendentals=6 * length * length * heads,
            bytes_accessed=16 * length * width),
    )(mask_row, q, k, v, kv_prev, kv_next)


def _backward_kernel(mask_ref, q_ref, k_ref, v_ref, kvp_ref, kvn_ref, g_ref, lse_ref, delta_ref,
                     dq_ref, prev_ref, next_ref, own_ref, *, heads, scale):
    length = q_ref.shape[0]
    width = q_ref.shape[1]
    row = lax.broadcasted_iota(jnp.int32, (3 * length, 1), 0)
    live = jnp.zeros((3 * length, 1), jnp.bool_)
    for c in range(3):
        live = live | ((row >= c * length) & (row < (c + 1) * length) & (mask_ref[c] > 0))

    def front(h):
        cols = slice(h * HSZ, (h + 1) * HSZ)
        q = q_ref[:, cols]
        g = g_ref[:, cols]
        keys, vals = _window(k_ref, v_ref, kvp_ref, kvn_ref, h)
        keys = jnp.concatenate(keys, axis=0)
        s_t = jnp.where(live, _nt(keys, q) * scale, NEGATIVE)
        dp_t = _nt(jnp.concatenate(vals, axis=0), g)
        return q, g, keys, s_t, dp_t

    ahead = [front(h) for h in range(min(LOOKAHEAD, heads))]
    for h in range(heads):
        cols = slice(h * HSZ, (h + 1) * HSZ)
        q, g, keys, s_t, dp_t = ahead.pop(0)
        if h + LOOKAHEAD < heads:
            ahead.append(front(h + LOOKAHEAD))
        p_t = jnp.exp(s_t - lse_ref[h:h + 1, :])
        ds_t = (p_t * (dp_t - delta_ref[h:h + 1, :])).astype(jnp.bfloat16)
        dq_ref[:, cols] = (_tn(ds_t, keys) * scale).astype(dq_ref.dtype)
        dk = _nn(ds_t, q) * scale
        dv = _nn(p_t.astype(jnp.bfloat16), g)
        for c, ref in enumerate((prev_ref, own_ref, next_ref)):
            blk = slice(c * length, (c + 1) * length)
            ref[:, cols] = dk[blk].astype(ref.dtype)
            ref[:, width + h * HSZ:width + (h + 1) * HSZ] = dv[blk].astype(ref.dtype)


def attend_backward(mask_row, q, k, v, kv_prev, kv_next, grad, lse, delta):
    length, width = q.shape
    heads = width // HSZ
    kern = functools.partial(_backward_kernel, heads=heads, scale=HSZ ** (-0.5))
    vmem = pl.BlockSpec(memory_space=pltpu.VMEM)
    sent = jax.ShapeDtypeStruct((length, 2 * width), jnp.bfloat16)
    return pl.pallas_call(
        kern,
        out_shape=(jax.ShapeDtypeStruct((length, width), jnp.bfloat16), sent, sent,
                   jax.ShapeDtypeStruct((length, 2 * width), jnp.float32)),
        in_specs=[pl.BlockSpec(memory_space=pltpu.SMEM)] + [vmem] * 8,
        out_specs=(vmem, vmem, vmem, vmem),
        cost_estimate=pl.CostEstimate(
            flops=30 * length * length * width, transcendentals=3 * length * length * heads,
            bytes_accessed=36 * length * width),
    )(mask_row, q, k, v, kv_prev, kv_next, grad, lse.T, delta.T)


def per_device(queries, key_rows, value_rows, view_mask, norm_gain, normed_grad):
    length = queries.shape[0]
    width = queries.shape[1]
    features = norm_gain.shape[0]
    position = lax.axis_index("ctx")
    part = lax.axis_index("tp")

    grad_tiles = tiles_to_heads(normed_grad, width)
    gain_local = lax.dynamic_slice_in_dim(norm_gain, part * width, width, 0)

    both = jnp.concatenate([key_rows, value_rows], axis=1)
    from_prev = passed_along(both, "ctx", 1)
    from_next = passed_along(both, "ctx", -1)
    mask_row = lax.dynamic_slice_in_dim(view_mask, position, 1, 0)[0]
    attended, log_total = attend_forward(mask_row, queries, key_rows, value_rows, from_prev, from_next)
    out_heads = split_heads(attended)

    values_f = attended.astype(jnp.float32)
    upstream = grad_tiles.astype(jnp.float32) * gain_local
    partial = jnp.stack(
        [jnp.sum(values_f * values_f, -1), jnp.sum(upstream * values_f, -1)], axis=-1
    )
    totals = tp_sum(partial)
    inverse = lax.rsqrt(totals[:, 0:1] / features + EPSILON)
    inner_mean = totals[:, 1:2] / features
    normed_heads = (values_f * inverse * gain_local).astype(jnp.bfloat16)
    normed = heads_to_tiles(normed_heads, normed_grad.shape[0])
    attended_grad = (
        inverse * upstream - values_f * inverse * inverse * inverse * inner_mean
    ).astype(jnp.bfloat16)

    grad_heads = split_heads(attended_grad)
    delta = jnp.sum(grad_heads.astype(jnp.float32) * out_heads.astype(jnp.float32), -1)
    query_grad, to_prev, to_next, own = attend_backward(
        mask_row, queries, key_rows, value_rows, from_prev, from_next, attended_grad, log_total, delta)
    total = own + passed_along(to_prev, "ctx", -1).astype(jnp.float32)
    total = total + passed_along(to_next, "ctx", 1).astype(jnp.float32)
    total = total.astype(jnp.bfloat16)
    return (normed, query_grad, total[:, :width], total[:, width:])

def solution(mesh):
    placed = (P("ctx", "tp"), P("ctx", "tp"), P("ctx", "tp"), P(), P(), P(("ctx", "tp"), None))
    return jax.shard_map(
        per_device,
        mesh=mesh,
        in_specs=placed,
        out_specs=(P(("ctx", "tp"), None), P("ctx", "tp"), P("ctx", "tp"), P("ctx", "tp")),
        check_vma=False,
    )
```

```python
import functools

import jax
import jax.numpy as jnp
from jax import lax
from jax.experimental import pallas as pl
from jax.experimental.pallas import tpu as pltpu
from jax.sharding import PartitionSpec as P

HSZ = 128
REACH = 2


NEGATIVE = -1e30
EPSILON = 1e-06
LOOKAHEAD = 3
STATS_SUM = "xor"
NG_MODE = "perm"
OUT_MODE = "perm"


def passed_along(x, axis, by):
    peers = lax.axis_size(axis)
    pairs = [(i, i + by) for i in range(peers) if 0 <= i + by < peers]
    return lax.ppermute(x, axis, pairs)


def split_heads(values):
    return values.reshape(values.shape[0], -1, HSZ)


def xor_flip(stacked, part, n):
    bits = n.bit_length() - 1
    view = stacked.reshape((2,) * bits + stacked.shape[1:])
    for b in range(bits):
        axis = bits - 1 - b
        view = jnp.where((part >> b) & 1 == 1, jnp.flip(view, axis), view)
    return view.reshape(stacked.shape)


def xor_exchange(stacked, n):
    bits = n.bit_length() - 1
    view = stacked.reshape((2,) * bits + stacked.shape[1:])
    for b in range(bits):
        axis = bits - 1 - b
        keep = lax.index_in_dim(view, 0, axis, keepdims=True)
        sent = lax.index_in_dim(view, 1, axis, keepdims=True)
        got = lax.ppermute(sent, "tp", [(i, i ^ (1 << b)) for i in range(n)])
        view = jnp.concatenate([keep, got], axis)
    return view.reshape(stacked.shape)


def power_of_two(n):
    return n & (n - 1) == 0


def tp_sum(stats):
    if STATS_SUM == "psum":
        return lax.psum(stats, "tp")
    peers = lax.axis_size("tp")
    if STATS_SUM == "xor" and power_of_two(peers):
        total = stats
        for b in range(peers.bit_length() - 1):
            total = total + lax.ppermute(total, "tp", [(i, i ^ (1 << b)) for i in range(peers)])
        return total
    if STATS_SUM == "a2a":
        spread = jnp.broadcast_to(stats[None], (peers,) + stats.shape)
        gathered = lax.all_to_all(spread, "tp", split_axis=0, concat_axis=0, tiled=True)
        return jnp.sum(gathered, 0)
    total = stats
    for shift in range(1, peers):
        total = total + lax.ppermute(stats, "tp", [(i, (i + shift) % peers) for i in range(peers)])
    return total


def rolled(pieces, part):
    n = len(pieces)
    ordered = jnp.stack([pieces[(-j) % n] for j in range(n)], 0)
    return jnp.roll(ordered, part, axis=0)


def tiles_to_heads(tile, width):
    n = lax.axis_size("tp")
    part = lax.axis_index("tp")
    if NG_MODE == "a2a":
        return lax.all_to_all(tile, "tp", split_axis=1, concat_axis=0, tiled=True)
    if NG_MODE == "xor" and power_of_two(n):
        groups = jnp.moveaxis(tile.reshape(tile.shape[0], n, width), 1, 0)
        got = xor_flip(xor_exchange(xor_flip(groups, part, n), n), part, n)
        return got.reshape(n * tile.shape[0], width)
    pieces = []
    for shift in range(n):
        dest = (part + shift) % n
        chunk = lax.dynamic_slice_in_dim(tile, dest * width, width, 1)
        if shift:
            chunk = lax.ppermute(chunk, "tp", [(i, (i + shift) % n) for i in range(n)])
        pieces.append(chunk)
    return rolled(pieces, part).reshape(n * tile.shape[0], width)


def heads_to_tiles(block, rows):
    n = lax.axis_size("tp")
    part = lax.axis_index("tp")
    if OUT_MODE == "a2a":
        return lax.all_to_all(block, "tp", split_axis=0, concat_axis=1, tiled=True)
    if OUT_MODE == "xor" and power_of_two(n):
        tiles = block.reshape(n, rows, block.shape[1])
        got = xor_flip(xor_exchange(xor_flip(tiles, part, n), n), part, n)
        return jnp.moveaxis(got, 0, 1).reshape(rows, -1)
    pieces = []
    for shift in range(n):
        dest = (part + shift) % n
        chunk = lax.dynamic_slice_in_dim(block, dest * rows, rows, 0)
        if shift:
            chunk = lax.ppermute(chunk, "tp", [(i, (i + shift) % n) for i in range(n)])
        pieces.append(chunk)
    ordered = rolled(pieces, part)
    return jnp.moveaxis(ordered, 0, 1).reshape(rows, -1)


def _nt(a, b):
    return lax.dot_general(a, b, (((1,), (1,)), ((), ())), preferred_element_type=jnp.float32)


def _nn(a, b):
    return lax.dot_general(a, b, (((1,), (0,)), ((), ())), preferred_element_type=jnp.float32)


def _tn(a, b):
    return lax.dot_general(a, b, (((0,), (0,)), ((), ())), preferred_element_type=jnp.float32)


def _scores(mask_ref, q, keys, scale):
    parts = []
    for c, k in enumerate(keys):
        s = _nt(q, k) * scale
        parts.append(jnp.where(mask_ref[c] > 0, s, NEGATIVE))
    return jnp.concatenate(parts, axis=1)


def _window(refs, h):
    k_ref, v_ref, kp_ref, vp_ref, kn_ref, vn_ref = refs
    cols = slice(h * HSZ, (h + 1) * HSZ)
    keys = [kp_ref[:, cols], k_ref[:, cols], kn_ref[:, cols]]
    values = [vp_ref[:, cols], v_ref[:, cols], vn_ref[:, cols]]
    return keys, values


def _group(heads):
    return max(g for g in (1, 2, 4) if heads % g == 0)


def _block_specs(length, group, steps):
    span = group * HSZ
    own = pl.BlockSpec((length, span), lambda j: (0, j))
    far = pl.BlockSpec((length, span), lambda j: (0, steps + j))
    rows = pl.BlockSpec((1, group, length), lambda j: (j, 0, 0))
    pair = pl.BlockSpec((2, length, span), lambda j: (0, 0, j))
    return own, far, rows, pair


def _forward_kernel(mask_ref, q_ref, k_ref, v_ref, kp_ref, vp_ref, kn_ref, vn_ref, out_ref, lse_ref, *,
                    heads, scale):
    refs = (k_ref, v_ref, kp_ref, vp_ref, kn_ref, vn_ref)
    length = q_ref.shape[0]
    row = lax.broadcasted_iota(jnp.int32, (3 * length, 1), 0)
    live = jnp.zeros((3 * length, 1), jnp.bool_)
    for c in range(3):
        live = live | ((row >= c * length) & (row < (c + 1) * length) & (mask_ref[c] > 0))

    def scores(h):
        keys, values = _window(refs, h)
        s_t = _nt(jnp.concatenate(keys, axis=0), q_ref[:, h * HSZ:(h + 1) * HSZ]) * scale
        return jnp.where(live, s_t, NEGATIVE), values

    ahead = [scores(h) for h in range(min(LOOKAHEAD, heads))]
    for h in range(heads):
        s_t, values = ahead.pop(0)
        if h + LOOKAHEAD < heads:
            ahead.append(scores(h + LOOKAHEAD))
        peak = jnp.max(s_t, 0, keepdims=True)
        lse = peak + jnp.log(jnp.sum(jnp.exp(s_t - peak), 0, keepdims=True))
        p_t = jnp.exp(s_t - lse).astype(jnp.bfloat16)
        v = jnp.concatenate(values, axis=0)
        out_ref[:, h * HSZ:(h + 1) * HSZ] = _tn(p_t, v).astype(out_ref.dtype)
        lse_ref[0, h:h + 1, :] = lse


def attend_forward(mask_row, q, k, v, kv_prev, kv_next):
    length, width = q.shape
    heads = width // HSZ
    group = _group(heads)
    steps = heads // group
    own, far, rows, _ = _block_specs(length, group, steps)
    return pl.pallas_call(
        functools.partial(_forward_kernel, heads=group, scale=HSZ ** (-0.5)),
        grid=(steps,),
        out_shape=(jax.ShapeDtypeStruct((length, width), jnp.bfloat16),
                   jax.ShapeDtypeStruct((steps, group, length), jnp.float32)),
        in_specs=[pl.BlockSpec(memory_space=pltpu.SMEM), own, own, own, own, far, own, far],
        out_specs=(own, rows),
        cost_estimate=pl.CostEstimate(
            flops=12 * length * length * width, transcendentals=6 * length * length * heads,
            bytes_accessed=16 * length * width),
    )(mask_row, q, k, v, kv_prev, kv_prev, kv_next, kv_next)


def _backward_kernel(mask_ref, q_ref, k_ref, v_ref, kp_ref, vp_ref, kn_ref, vn_ref, g_ref, lse_ref, delta_ref,
                     dq_ref, prev_ref, next_ref, own_ref, *, heads, scale):
    refs = (k_ref, v_ref, kp_ref, vp_ref, kn_ref, vn_ref)
    length = q_ref.shape[0]
    width = q_ref.shape[1]
    row = lax.broadcasted_iota(jnp.int32, (3 * length, 1), 0)
    live = jnp.zeros((3 * length, 1), jnp.bool_)
    for c in range(3):
        live = live | ((row >= c * length) & (row < (c + 1) * length) & (mask_ref[c] > 0))

    def front(h):
        cols = slice(h * HSZ, (h + 1) * HSZ)
        q = q_ref[:, cols]
        g = g_ref[:, cols]
        keys, vals = _window(refs, h)
        keys = jnp.concatenate(keys, axis=0)
        s_t = jnp.where(live, _nt(keys, q) * scale, NEGATIVE)
        dp_t = _nt(jnp.concatenate(vals, axis=0), g)
        return q, g, keys, s_t, dp_t

    ahead = [front(h) for h in range(min(LOOKAHEAD, heads))]
    for h in range(heads):
        cols = slice(h * HSZ, (h + 1) * HSZ)
        q, g, keys, s_t, dp_t = ahead.pop(0)
        if h + LOOKAHEAD < heads:
            ahead.append(front(h + LOOKAHEAD))
        p_t = jnp.exp(s_t - lse_ref[0, h:h + 1, :])
        ds_t = (p_t * (dp_t - delta_ref[0, h:h + 1, :])).astype(jnp.bfloat16)
        dq_ref[:, cols] = (_tn(ds_t, keys) * scale).astype(dq_ref.dtype)
        dk = _nn(ds_t, q) * scale
        dv = _nn(p_t.astype(jnp.bfloat16), g)
        for c, ref in enumerate((prev_ref, own_ref, next_ref)):
            blk = slice(c * length, (c + 1) * length)
            ref[0, :, cols] = dk[blk].astype(ref.dtype)
            ref[1, :, cols] = dv[blk].astype(ref.dtype)


def attend_backward(mask_row, q, k, v, kv_prev, kv_next, grad, lse, delta):
    length, width = q.shape
    heads = width // HSZ
    group = _group(heads)
    steps = heads // group
    own, far, rows, pair = _block_specs(length, group, steps)
    sent = jax.ShapeDtypeStruct((2, length, width), jnp.bfloat16)
    return pl.pallas_call(
        functools.partial(_backward_kernel, heads=group, scale=HSZ ** (-0.5)),
        grid=(steps,),
        out_shape=(jax.ShapeDtypeStruct((length, width), jnp.bfloat16), sent, sent,
                   jax.ShapeDtypeStruct((2, length, width), jnp.float32)),
        in_specs=[pl.BlockSpec(memory_space=pltpu.SMEM), own, own, own, own, far, own, far, own, rows, rows],
        out_specs=(own, pair, pair, pair),
        cost_estimate=pl.CostEstimate(
            flops=30 * length * length * width, transcendentals=3 * length * length * heads,
            bytes_accessed=36 * length * width),
    )(mask_row, q, k, v, kv_prev, kv_prev, kv_next, kv_next, grad, lse, delta.T.reshape(lse.shape))


def per_device(queries, key_rows, value_rows, view_mask, norm_gain, normed_grad):
    length = queries.shape[0]
    width = queries.shape[1]
    features = norm_gain.shape[0]
    position = lax.axis_index("ctx")
    part = lax.axis_index("tp")

    grad_tiles = tiles_to_heads(normed_grad, width)
    gain_local = lax.dynamic_slice_in_dim(norm_gain, part * width, width, 0)

    both = jnp.concatenate([key_rows, value_rows], axis=1)
    from_prev = passed_along(both, "ctx", 1)
    from_next = passed_along(both, "ctx", -1)
    mask_row = lax.dynamic_slice_in_dim(view_mask, position, 1, 0)[0]
    attended, log_total = attend_forward(mask_row, queries, key_rows, value_rows, from_prev, from_next)
    out_heads = split_heads(attended)

    values_f = attended.astype(jnp.float32)
    upstream = grad_tiles.astype(jnp.float32) * gain_local
    partial = jnp.stack(
        [jnp.sum(values_f * values_f, -1), jnp.sum(upstream * values_f, -1)], axis=-1
    )
    totals = tp_sum(partial)
    inverse = lax.rsqrt(totals[:, 0:1] / features + EPSILON)
    inner_mean = totals[:, 1:2] / features
    normed_heads = (values_f * inverse * gain_local).astype(jnp.bfloat16)
    normed = heads_to_tiles(normed_heads, normed_grad.shape[0])
    attended_grad = (
        inverse * upstream - values_f * inverse * inverse * inverse * inner_mean
    ).astype(jnp.bfloat16)

    grad_heads = split_heads(attended_grad)
    delta = jnp.sum(grad_heads.astype(jnp.float32) * out_heads.astype(jnp.float32), -1)
    query_grad, to_prev, to_next, own = attend_backward(
        mask_row, queries, key_rows, value_rows, from_prev, from_next, attended_grad, log_total, delta)
    total = own + passed_along(to_prev, "ctx", -1).astype(jnp.float32)
    total = total + passed_along(to_next, "ctx", 1).astype(jnp.float32)
    total = total.astype(jnp.bfloat16)
    return (normed, query_grad, total[0], total[1])


def solution(mesh):
    placed = (P("ctx", "tp"), P("ctx", "tp"), P("ctx", "tp"), P(), P(), P(("ctx", "tp"), None))
    return jax.shard_map(
        per_device,
        mesh=mesh,
        in_specs=placed,
        out_specs=(P(("ctx", "tp"), None), P("ctx", "tp"), P("ctx", "tp"), P("ctx", "tp")),
        check_vma=False,
    )
```

```python
import functools

import jax
import jax.numpy as jnp
from jax import lax
from jax.experimental import pallas as pl
from jax.experimental.pallas import tpu as pltpu
from jax.sharding import PartitionSpec as P

HSZ = 128
REACH = 2


NEGATIVE = -1e30
EPSILON = 1e-06
LOOKAHEAD = 3
STATS_SUM = "xor"
NG_MODE = "perm"
OUT_MODE = "perm"


def passed_along(x, axis, by):
    peers = lax.axis_size(axis)
    pairs = [(i, i + by) for i in range(peers) if 0 <= i + by < peers]
    return lax.ppermute(x, axis, pairs)


def split_heads(values):
    return values.reshape(values.shape[0], -1, HSZ)


def xor_flip(stacked, part, n):
    bits = n.bit_length() - 1
    view = stacked.reshape((2,) * bits + stacked.shape[1:])
    for b in range(bits):
        axis = bits - 1 - b
        view = jnp.where((part >> b) & 1 == 1, jnp.flip(view, axis), view)
    return view.reshape(stacked.shape)


def xor_exchange(stacked, n):
    bits = n.bit_length() - 1
    view = stacked.reshape((2,) * bits + stacked.shape[1:])
    for b in range(bits):
        axis = bits - 1 - b
        keep = lax.index_in_dim(view, 0, axis, keepdims=True)
        sent = lax.index_in_dim(view, 1, axis, keepdims=True)
        got = lax.ppermute(sent, "tp", [(i, i ^ (1 << b)) for i in range(n)])
        view = jnp.concatenate([keep, got], axis)
    return view.reshape(stacked.shape)


def power_of_two(n):
    return n & (n - 1) == 0


def tp_sum(stats):
    if STATS_SUM == "psum":
        return lax.psum(stats, "tp")
    peers = lax.axis_size("tp")
    if STATS_SUM == "xor" and power_of_two(peers):
        total = stats
        for b in range(peers.bit_length() - 1):
            total = total + lax.ppermute(total, "tp", [(i, i ^ (1 << b)) for i in range(peers)])
        return total
    if STATS_SUM == "a2a":
        spread = jnp.broadcast_to(stats[None], (peers,) + stats.shape)
        gathered = lax.all_to_all(spread, "tp", split_axis=0, concat_axis=0, tiled=True)
        return jnp.sum(gathered, 0)
    total = stats
    for shift in range(1, peers):
        total = total + lax.ppermute(stats, "tp", [(i, (i + shift) % peers) for i in range(peers)])
    return total


def rolled(pieces, part):
    n = len(pieces)
    ordered = jnp.stack([pieces[(-j) % n] for j in range(n)], 0)
    return jnp.roll(ordered, part, axis=0)


def tiles_to_heads(tile, width):
    n = lax.axis_size("tp")
    part = lax.axis_index("tp")
    if NG_MODE == "a2a":
        return lax.all_to_all(tile, "tp", split_axis=1, concat_axis=0, tiled=True)
    if NG_MODE == "xor" and power_of_two(n):
        groups = jnp.moveaxis(tile.reshape(tile.shape[0], n, width), 1, 0)
        got = xor_flip(xor_exchange(xor_flip(groups, part, n), n), part, n)
        return got.reshape(n * tile.shape[0], width)
    pieces = []
    for shift in range(n):
        dest = (part + shift) % n
        chunk = lax.dynamic_slice_in_dim(tile, dest * width, width, 1)
        if shift:
            chunk = lax.ppermute(chunk, "tp", [(i, (i + shift) % n) for i in range(n)])
        pieces.append(chunk)
    return rolled(pieces, part).reshape(n * tile.shape[0], width)


def heads_to_tiles(block, rows):
    n = lax.axis_size("tp")
    part = lax.axis_index("tp")
    if OUT_MODE == "a2a":
        return lax.all_to_all(block, "tp", split_axis=0, concat_axis=1, tiled=True)
    if OUT_MODE == "xor" and power_of_two(n):
        tiles = block.reshape(n, rows, block.shape[1])
        got = xor_flip(xor_exchange(xor_flip(tiles, part, n), n), part, n)
        return jnp.moveaxis(got, 0, 1).reshape(rows, -1)
    pieces = []
    for shift in range(n):
        dest = (part + shift) % n
        chunk = lax.dynamic_slice_in_dim(block, dest * rows, rows, 0)
        if shift:
            chunk = lax.ppermute(chunk, "tp", [(i, (i + shift) % n) for i in range(n)])
        pieces.append(chunk)
    ordered = rolled(pieces, part)
    return jnp.moveaxis(ordered, 0, 1).reshape(rows, -1)


def _nt(a, b):
    return lax.dot_general(a, b, (((1,), (1,)), ((), ())), preferred_element_type=jnp.float32)


def _nn(a, b):
    return lax.dot_general(a, b, (((1,), (0,)), ((), ())), preferred_element_type=jnp.float32)


def _tn(a, b):
    return lax.dot_general(a, b, (((0,), (0,)), ((), ())), preferred_element_type=jnp.float32)


def _scores(mask_ref, q, keys, scale):
    parts = []
    for c, k in enumerate(keys):
        s = _nt(q, k) * scale
        parts.append(jnp.where(mask_ref[c] > 0, s, NEGATIVE))
    return jnp.concatenate(parts, axis=1)


def _window(refs, h):
    k_ref, v_ref, kp_ref, vp_ref, kn_ref, vn_ref = refs
    cols = slice(h * HSZ, (h + 1) * HSZ)
    keys = [kp_ref[:, cols], k_ref[:, cols], kn_ref[:, cols]]
    values = [vp_ref[:, cols], v_ref[:, cols], vn_ref[:, cols]]
    return keys, values


def _group(heads):
    return max(g for g in (1, 2, 4) if heads % g == 0)


def _block_specs(length, group, steps):
    span = group * HSZ
    own = pl.BlockSpec((length, span), lambda j: (0, j))
    far = pl.BlockSpec((length, span), lambda j: (0, steps + j))
    rows = pl.BlockSpec((1, group, length), lambda j: (j, 0, 0))
    pair = pl.BlockSpec((2, length, span), lambda j: (0, 0, j))
    return own, far, rows, pair


def _forward_kernel(mask_ref, q_ref, k_ref, v_ref, kp_ref, vp_ref, kn_ref, vn_ref, out_ref, lse_ref, *,
                    heads, scale):
    refs = (k_ref, v_ref, kp_ref, vp_ref, kn_ref, vn_ref)
    length = q_ref.shape[0]
    row = lax.broadcasted_iota(jnp.int32, (3 * length, 1), 0)
    live = jnp.zeros((3 * length, 1), jnp.bool_)
    for c in range(3):
        live = live | ((row >= c * length) & (row < (c + 1) * length) & (mask_ref[c] > 0))

    def scores(h):
        keys, values = _window(refs, h)
        s_t = _nt(jnp.concatenate(keys, axis=0), q_ref[:, h * HSZ:(h + 1) * HSZ]) * scale
        return jnp.where(live, s_t, NEGATIVE), values

    ahead = [scores(h) for h in range(min(LOOKAHEAD, heads))]
    for h in range(heads):
        s_t, values = ahead.pop(0)
        if h + LOOKAHEAD < heads:
            ahead.append(scores(h + LOOKAHEAD))
        peak = jnp.max(s_t, 0, keepdims=True)
        lse = peak + jnp.log(jnp.sum(jnp.exp(s_t - peak), 0, keepdims=True))
        p_t = jnp.exp(s_t - lse).astype(jnp.bfloat16)
        v = jnp.concatenate(values, axis=0)
        out_ref[:, h * HSZ:(h + 1) * HSZ] = _tn(p_t, v).astype(out_ref.dtype)
        lse_ref[0, h:h + 1, :] = lse


def attend_forward(mask_row, q, k, v, kv_prev, kv_next):
    length, width = q.shape
    heads = width // HSZ
    group = _group(heads)
    steps = heads // group
    own, far, rows, _ = _block_specs(length, group, steps)
    return pl.pallas_call(
        functools.partial(_forward_kernel, heads=group, scale=HSZ ** (-0.5)),
        grid=(steps,),
        out_shape=(jax.ShapeDtypeStruct((length, width), jnp.bfloat16),
                   jax.ShapeDtypeStruct((steps, group, length), jnp.float32)),
        in_specs=[pl.BlockSpec(memory_space=pltpu.SMEM), own, own, own, own, far, own, far],
        out_specs=(own, rows),
        cost_estimate=pl.CostEstimate(
            flops=12 * length * length * width, transcendentals=6 * length * length * heads,
            bytes_accessed=16 * length * width),
    )(mask_row, q, k, v, kv_prev, kv_prev, kv_next, kv_next)


def _backward_kernel(mask_ref, q_ref, k_ref, v_ref, kp_ref, vp_ref, kn_ref, vn_ref, t_ref, o_ref, gain_ref,
                     norm_ref, lse_ref, dq_ref, prev_ref, next_ref, own_ref, *, heads, scale):
    refs = (k_ref, v_ref, kp_ref, vp_ref, kn_ref, vn_ref)
    length = q_ref.shape[0]
    width = q_ref.shape[1]
    row = lax.broadcasted_iota(jnp.int32, (3 * length, 1), 0)
    live = jnp.zeros((3 * length, 1), jnp.bool_)
    for c in range(3):
        live = live | ((row >= c * length) & (row < (c + 1) * length) & (mask_ref[c] > 0))

    def front(h):
        cols = slice(h * HSZ, (h + 1) * HSZ)
        q = q_ref[:, cols]
        inverse = norm_ref[:, 0:1]
        inner_mean = norm_ref[:, 1:2]
        out_f = o_ref[:, cols].astype(jnp.float32)
        upstream = t_ref[:, cols].astype(jnp.float32) * gain_ref[:, cols]
        g = (inverse * upstream - out_f * inverse * inverse * inverse * inner_mean).astype(jnp.bfloat16)
        delta = jnp.sum((g.astype(jnp.float32) * out_f).T, 0, keepdims=True)
        keys, vals = _window(refs, h)
        keys = jnp.concatenate(keys, axis=0)
        s_t = jnp.where(live, _nt(keys, q) * scale, NEGATIVE)
        dp_t = _nt(jnp.concatenate(vals, axis=0), g)
        return q, g, keys, s_t, dp_t, delta

    ahead = [front(h) for h in range(min(LOOKAHEAD, heads))]
    for h in range(heads):
        cols = slice(h * HSZ, (h + 1) * HSZ)
        q, g, keys, s_t, dp_t, delta = ahead.pop(0)
        if h + LOOKAHEAD < heads:
            ahead.append(front(h + LOOKAHEAD))
        p_t = jnp.exp(s_t - lse_ref[0, h:h + 1, :])
        ds_t = (p_t * (dp_t - delta)).astype(jnp.bfloat16)
        dq_ref[:, cols] = (_tn(ds_t, keys) * scale).astype(dq_ref.dtype)
        dk = _nn(ds_t, q) * scale
        dv = _nn(p_t.astype(jnp.bfloat16), g)
        for c, ref in enumerate((prev_ref, own_ref, next_ref)):
            blk = slice(c * length, (c + 1) * length)
            ref[0, :, cols] = dk[blk].astype(ref.dtype)
            ref[1, :, cols] = dv[blk].astype(ref.dtype)


def attend_backward(mask_row, q, k, v, kv_prev, kv_next, grad_tiles, attended, gain, norm, lse):
    length, width = q.shape
    heads = width // HSZ
    group = _group(heads)
    steps = heads // group
    own, far, rows, pair = _block_specs(length, group, steps)
    sent = jax.ShapeDtypeStruct((2, length, width), jnp.bfloat16)
    return pl.pallas_call(
        functools.partial(_backward_kernel, heads=group, scale=HSZ ** (-0.5)),
        grid=(steps,),
        out_shape=(jax.ShapeDtypeStruct((length, width), jnp.bfloat16), sent, sent,
                   jax.ShapeDtypeStruct((2, length, width), jnp.float32)),
        in_specs=[pl.BlockSpec(memory_space=pltpu.SMEM), own, own, own, own, far, own, far, own, own,
                  pl.BlockSpec((1, group * HSZ), lambda j: (0, j)), pl.BlockSpec((length, 2), lambda j: (0, 0)),
                  rows],
        out_specs=(own, pair, pair, pair),
        cost_estimate=pl.CostEstimate(
            flops=30 * length * length * width, transcendentals=3 * length * length * heads,
            bytes_accessed=36 * length * width),
    )(mask_row, q, k, v, kv_prev, kv_prev, kv_next, kv_next, grad_tiles, attended, gain, norm, lse)


def per_device(queries, key_rows, value_rows, view_mask, norm_gain, normed_grad):
    length = queries.shape[0]
    width = queries.shape[1]
    features = norm_gain.shape[0]
    position = lax.axis_index("ctx")
    part = lax.axis_index("tp")

    grad_tiles = tiles_to_heads(normed_grad, width)
    gain_local = lax.dynamic_slice_in_dim(norm_gain, part * width, width, 0)

    both = jnp.concatenate([key_rows, value_rows], axis=1)
    from_prev = passed_along(both, "ctx", 1)
    from_next = passed_along(both, "ctx", -1)
    mask_row = lax.dynamic_slice_in_dim(view_mask, position, 1, 0)[0]
    attended, log_total = attend_forward(mask_row, queries, key_rows, value_rows, from_prev, from_next)

    values_f = attended.astype(jnp.float32)
    upstream = grad_tiles.astype(jnp.float32) * gain_local
    partial = jnp.stack(
        [jnp.sum(values_f * values_f, -1), jnp.sum(upstream * values_f, -1)], axis=-1
    )
    totals = tp_sum(partial)
    inverse = lax.rsqrt(totals[:, 0:1] / features + EPSILON)
    inner_mean = totals[:, 1:2] / features
    normed_heads = (values_f * inverse * gain_local).astype(jnp.bfloat16)
    normed = heads_to_tiles(normed_heads, normed_grad.shape[0])
    norm = jnp.concatenate([inverse, inner_mean], axis=1)
    query_grad, to_prev, to_next, own = attend_backward(
        mask_row, queries, key_rows, value_rows, from_prev, from_next, grad_tiles, attended,
        gain_local[None, :], norm, log_total)
    total = own + passed_along(to_prev, "ctx", -1).astype(jnp.float32)
    total = total + passed_along(to_next, "ctx", 1).astype(jnp.float32)
    total = total.astype(jnp.bfloat16)
    return (normed, query_grad, total[0], total[1])


def solution(mesh):
    placed = (P("ctx", "tp"), P("ctx", "tp"), P("ctx", "tp"), P(), P(), P(("ctx", "tp"), None))
    return jax.shard_map(
        per_device,
        mesh=mesh,
        in_specs=placed,
        out_specs=(P(("ctx", "tp"), None), P("ctx", "tp"), P("ctx", "tp"), P("ctx", "tp")),
        check_vma=False,
    )
```

```python
import functools

import jax
import jax.numpy as jnp
from jax import lax
from jax.experimental import pallas as pl
from jax.experimental.pallas import tpu as pltpu
from jax.sharding import PartitionSpec as P

HSZ = 128
REACH = 2


NEGATIVE = -1e30
EPSILON = 1e-06
LOOKAHEAD = 3
STATS_SUM = "perm"
NG_MODE = "perm"
OUT_MODE = "perm"


def passed_along(x, axis, by):
    peers = lax.axis_size(axis)
    pairs = [(i, i + by) for i in range(peers) if 0 <= i + by < peers]
    return lax.ppermute(x, axis, pairs)


def split_heads(values):
    return values.reshape(values.shape[0], -1, HSZ)


def xor_flip(stacked, part, n):
    bits = n.bit_length() - 1
    view = stacked.reshape((2,) * bits + stacked.shape[1:])
    for b in range(bits):
        axis = bits - 1 - b
        view = jnp.where((part >> b) & 1 == 1, jnp.flip(view, axis), view)
    return view.reshape(stacked.shape)


def xor_exchange(stacked, n):
    bits = n.bit_length() - 1
    view = stacked.reshape((2,) * bits + stacked.shape[1:])
    for b in range(bits):
        axis = bits - 1 - b
        keep = lax.index_in_dim(view, 0, axis, keepdims=True)
        sent = lax.index_in_dim(view, 1, axis, keepdims=True)
        got = lax.ppermute(sent, "tp", [(i, i ^ (1 << b)) for i in range(n)])
        view = jnp.concatenate([keep, got], axis)
    return view.reshape(stacked.shape)


def power_of_two(n):
    return n & (n - 1) == 0


def tp_sum(stats):
    if STATS_SUM == "psum":
        return lax.psum(stats, "tp")
    peers = lax.axis_size("tp")
    if STATS_SUM == "xor" and power_of_two(peers):
        total = stats
        for b in range(peers.bit_length() - 1):
            total = total + lax.ppermute(total, "tp", [(i, i ^ (1 << b)) for i in range(peers)])
        return total
    if STATS_SUM == "a2a":
        spread = jnp.broadcast_to(stats[None], (peers,) + stats.shape)
        gathered = lax.all_to_all(spread, "tp", split_axis=0, concat_axis=0, tiled=True)
        return jnp.sum(gathered, 0)
    total = stats
    for shift in range(1, peers):
        total = total + lax.ppermute(stats, "tp", [(i, (i + shift) % peers) for i in range(peers)])
    return total


def rolled(pieces, part):
    n = len(pieces)
    ordered = jnp.stack([pieces[(-j) % n] for j in range(n)], 0)
    return jnp.roll(ordered, part, axis=0)


def tiles_to_heads(tile, width):
    n = lax.axis_size("tp")
    part = lax.axis_index("tp")
    if NG_MODE == "a2a":
        return lax.all_to_all(tile, "tp", split_axis=1, concat_axis=0, tiled=True)
    if NG_MODE == "xor" and power_of_two(n):
        groups = jnp.moveaxis(tile.reshape(tile.shape[0], n, width), 1, 0)
        got = xor_flip(xor_exchange(xor_flip(groups, part, n), n), part, n)
        return got.reshape(n * tile.shape[0], width)
    pieces = []
    for shift in range(n):
        dest = (part + shift) % n
        chunk = lax.dynamic_slice_in_dim(tile, dest * width, width, 1)
        if shift:
            chunk = lax.ppermute(chunk, "tp", [(i, (i + shift) % n) for i in range(n)])
        pieces.append(chunk)
    return rolled(pieces, part).reshape(n * tile.shape[0], width)


def heads_to_tiles(block, rows):
    n = lax.axis_size("tp")
    part = lax.axis_index("tp")
    if OUT_MODE == "a2a":
        return lax.all_to_all(block, "tp", split_axis=0, concat_axis=1, tiled=True)
    if OUT_MODE == "xor" and power_of_two(n):
        tiles = block.reshape(n, rows, block.shape[1])
        got = xor_flip(xor_exchange(xor_flip(tiles, part, n), n), part, n)
        return jnp.moveaxis(got, 0, 1).reshape(rows, -1)
    pieces = []
    for shift in range(n):
        dest = (part + shift) % n
        chunk = lax.dynamic_slice_in_dim(block, dest * rows, rows, 0)
        if shift:
            chunk = lax.ppermute(chunk, "tp", [(i, (i + shift) % n) for i in range(n)])
        pieces.append(chunk)
    ordered = rolled(pieces, part)
    return jnp.moveaxis(ordered, 0, 1).reshape(rows, -1)


def _nt(a, b):
    return lax.dot_general(a, b, (((1,), (1,)), ((), ())), preferred_element_type=jnp.float32)


def _nn(a, b):
    return lax.dot_general(a, b, (((1,), (0,)), ((), ())), preferred_element_type=jnp.float32)


def _tn(a, b):
    return lax.dot_general(a, b, (((0,), (0,)), ((), ())), preferred_element_type=jnp.float32)


def _scores(mask_ref, q, keys, scale):
    parts = []
    for c, k in enumerate(keys):
        s = _nt(q, k) * scale
        parts.append(jnp.where(mask_ref[c] > 0, s, NEGATIVE))
    return jnp.concatenate(parts, axis=1)


def _window(refs, h):
    k_ref, v_ref, kp_ref, vp_ref, kn_ref, vn_ref = refs
    cols = slice(h * HSZ, (h + 1) * HSZ)
    keys = [kp_ref[:, cols], k_ref[:, cols], kn_ref[:, cols]]
    values = [vp_ref[:, cols], v_ref[:, cols], vn_ref[:, cols]]
    return keys, values


def _group(heads):
    return max(g for g in (1, 2, 4) if heads % g == 0)


def _block_specs(length, group, steps):
    span = group * HSZ
    own = pl.BlockSpec((length, span), lambda j: (0, j))
    far = pl.BlockSpec((length, span), lambda j: (0, steps + j))
    rows = pl.BlockSpec((1, group, length), lambda j: (j, 0, 0))
    pair = pl.BlockSpec((2, length, span), lambda j: (0, 0, j))
    return own, far, rows, pair


def _forward_kernel(mask_ref, q_ref, k_ref, v_ref, kp_ref, vp_ref, kn_ref, vn_ref, out_ref, lse_ref, *,
                    heads, scale):
    refs = (k_ref, v_ref, kp_ref, vp_ref, kn_ref, vn_ref)
    length = q_ref.shape[0]
    row = lax.broadcasted_iota(jnp.int32, (3 * length, 1), 0)
    live = jnp.zeros((3 * length, 1), jnp.bool_)
    for c in range(3):
        live = live | ((row >= c * length) & (row < (c + 1) * length) & (mask_ref[c] > 0))

    def scores(h):
        keys, values = _window(refs, h)
        s_t = _nt(jnp.concatenate(keys, axis=0), q_ref[:, h * HSZ:(h + 1) * HSZ]) * scale
        return jnp.where(live, s_t, NEGATIVE), values

    ahead = [scores(h) for h in range(min(LOOKAHEAD, heads))]
    for h in range(heads):
        s_t, values = ahead.pop(0)
        if h + LOOKAHEAD < heads:
            ahead.append(scores(h + LOOKAHEAD))
        peak = jnp.max(s_t, 0, keepdims=True)
        lse = peak + jnp.log(jnp.sum(jnp.exp(s_t - peak), 0, keepdims=True))
        p_t = jnp.exp(s_t - lse).astype(jnp.bfloat16)
        v = jnp.concatenate(values, axis=0)
        out_ref[:, h * HSZ:(h + 1) * HSZ] = _tn(p_t, v).astype(out_ref.dtype)
        lse_ref[0, h:h + 1, :] = lse


def attend_forward(mask_row, q, k, v, kv_prev, kv_next):
    length, width = q.shape
    heads = width // HSZ
    group = _group(heads)
    steps = heads // group
    own, far, rows, _ = _block_specs(length, group, steps)
    return pl.pallas_call(
        functools.partial(_forward_kernel, heads=group, scale=HSZ ** (-0.5)),
        grid=(steps,),
        out_shape=(jax.ShapeDtypeStruct((length, width), jnp.bfloat16),
                   jax.ShapeDtypeStruct((steps, group, length), jnp.float32)),
        in_specs=[pl.BlockSpec(memory_space=pltpu.SMEM), own, own, own, own, far, own, far],
        out_specs=(own, rows),
        cost_estimate=pl.CostEstimate(
            flops=12 * length * length * width, transcendentals=6 * length * length * heads,
            bytes_accessed=16 * length * width),
    )(mask_row, q, k, v, kv_prev, kv_prev, kv_next, kv_next)


def _backward_kernel(mask_ref, q_ref, k_ref, v_ref, kp_ref, vp_ref, kn_ref, vn_ref, t_ref, o_ref, gain_ref,
                     norm_ref, lse_ref, dq_ref, prev_ref, next_ref, own_ref, *, heads, scale):
    refs = (k_ref, v_ref, kp_ref, vp_ref, kn_ref, vn_ref)
    length = q_ref.shape[0]
    width = q_ref.shape[1]
    row = lax.broadcasted_iota(jnp.int32, (3 * length, 1), 0)
    live = jnp.zeros((3 * length, 1), jnp.bool_)
    for c in range(3):
        live = live | ((row >= c * length) & (row < (c + 1) * length) & (mask_ref[c] > 0))

    def front(h):
        cols = slice(h * HSZ, (h + 1) * HSZ)
        q = q_ref[:, cols]
        inverse = norm_ref[:, 0:1]
        inner_mean = norm_ref[:, 1:2]
        out_f = o_ref[:, cols].astype(jnp.float32)
        upstream = t_ref[:, cols].astype(jnp.float32) * gain_ref[:, cols]
        g = (inverse * upstream - out_f * inverse * inverse * inverse * inner_mean).astype(jnp.bfloat16)
        delta = jnp.sum((g.astype(jnp.float32) * out_f).T, 0, keepdims=True)
        keys, vals = _window(refs, h)
        keys = jnp.concatenate(keys, axis=0)
        s_t = jnp.where(live, _nt(keys, q) * scale, NEGATIVE)
        dp_t = _nt(jnp.concatenate(vals, axis=0), g)
        return q, g, keys, s_t, dp_t, delta

    ahead = [front(h) for h in range(min(LOOKAHEAD, heads))]
    for h in range(heads):
        cols = slice(h * HSZ, (h + 1) * HSZ)
        q, g, keys, s_t, dp_t, delta = ahead.pop(0)
        if h + LOOKAHEAD < heads:
            ahead.append(front(h + LOOKAHEAD))
        p_t = jnp.exp(s_t - lse_ref[0, h:h + 1, :])
        ds_t = (p_t * (dp_t - delta)).astype(jnp.bfloat16)
        dq_ref[:, cols] = (_tn(ds_t, keys) * scale).astype(dq_ref.dtype)
        dk = _nn(ds_t, q) * scale
        dv = _nn(p_t.astype(jnp.bfloat16), g)
        for c, ref in enumerate((prev_ref, own_ref, next_ref)):
            blk = slice(c * length, (c + 1) * length)
            ref[0, :, cols] = dk[blk].astype(ref.dtype)
            ref[1, :, cols] = dv[blk].astype(ref.dtype)


def attend_backward(mask_row, q, k, v, kv_prev, kv_next, grad_tiles, attended, gain, norm, lse):
    length, width = q.shape
    heads = width // HSZ
    group = _group(heads)
    steps = heads // group
    own, far, rows, pair = _block_specs(length, group, steps)
    sent = jax.ShapeDtypeStruct((2, length, width), jnp.bfloat16)
    return pl.pallas_call(
        functools.partial(_backward_kernel, heads=group, scale=HSZ ** (-0.5)),
        grid=(steps,),
        out_shape=(jax.ShapeDtypeStruct((length, width), jnp.bfloat16), sent, sent,
                   jax.ShapeDtypeStruct((2, length, width), jnp.float32)),
        in_specs=[pl.BlockSpec(memory_space=pltpu.SMEM), own, own, own, own, far, own, far, own, own,
                  pl.BlockSpec((1, group * HSZ), lambda j: (0, j)), pl.BlockSpec((length, 2), lambda j: (0, 0)),
                  rows],
        out_specs=(own, pair, pair, pair),
        cost_estimate=pl.CostEstimate(
            flops=30 * length * length * width, transcendentals=3 * length * length * heads,
            bytes_accessed=36 * length * width),
    )(mask_row, q, k, v, kv_prev, kv_prev, kv_next, kv_next, grad_tiles, attended, gain, norm, lse)


def per_device(queries, key_rows, value_rows, view_mask, norm_gain, normed_grad):
    length = queries.shape[0]
    width = queries.shape[1]
    features = norm_gain.shape[0]
    position = lax.axis_index("ctx")
    part = lax.axis_index("tp")

    grad_tiles = tiles_to_heads(normed_grad, width)
    gain_local = lax.dynamic_slice_in_dim(norm_gain, part * width, width, 0)

    both = jnp.concatenate([key_rows, value_rows], axis=1)
    from_prev = passed_along(both, "ctx", 1)
    from_next = passed_along(both, "ctx", -1)
    mask_row = lax.dynamic_slice_in_dim(view_mask, position, 1, 0)[0]
    attended, log_total = attend_forward(mask_row, queries, key_rows, value_rows, from_prev, from_next)

    values_f = attended.astype(jnp.float32)
    upstream = grad_tiles.astype(jnp.float32) * gain_local
    partial = jnp.stack(
        [jnp.sum(values_f * values_f, -1), jnp.sum(upstream * values_f, -1)], axis=-1
    )
    totals = tp_sum(partial)
    inverse = lax.rsqrt(totals[:, 0:1] / features + EPSILON)
    inner_mean = totals[:, 1:2] / features
    normed_heads = (values_f * inverse * gain_local).astype(jnp.bfloat16)
    normed = heads_to_tiles(normed_heads, normed_grad.shape[0])
    norm = jnp.concatenate([inverse, inner_mean], axis=1)
    query_grad, to_prev, to_next, own = attend_backward(
        mask_row, queries, key_rows, value_rows, from_prev, from_next, grad_tiles, attended,
        gain_local[None, :], norm, log_total)
    total = own + passed_along(to_prev, "ctx", -1).astype(jnp.float32)
    total = total + passed_along(to_next, "ctx", 1).astype(jnp.float32)
    total = total.astype(jnp.bfloat16)
    return (normed, query_grad, total[0], total[1])


def solution(mesh):
    placed = (P("ctx", "tp"), P("ctx", "tp"), P("ctx", "tp"), P(), P(), P(("ctx", "tp"), None))
    return jax.shard_map(
        per_device,
        mesh=mesh,
        in_specs=placed,
        out_specs=(P(("ctx", "tp"), None), P("ctx", "tp"), P("ctx", "tp"), P("ctx", "tp")),
        check_vma=False,
    )
```
